32 devices in a mesh: seq: 8 (over z, x), tp: 4 (over y, core).
Axes of the slice: x: 2, y: 2, z: 4, core: 2. Of those that a mesh axis runs over, the one named last changes fastest.
Arguments:
- query_in: bfloat16 [4096, 4096], P('seq', 'tp'), may hold values from -6 to 6
- key_in: bfloat16 [4096, 4096], P('seq', 'tp'), may hold values from -6 to 6
- value_in: bfloat16 [4096, 4096], P('seq', 'tp'), may hold values from -6 to 6
- feature_taps: float32 [7, 3, 4096], P(None, None, 'tp'), may hold values from -2 to 2
- filter_taps: bfloat16 [256, 128], P('tp'), may hold values from -0.5 to 0.5
- out_weight: bfloat16 [4096, 4096], P('tp'), may hold values from -0.09375 to 0.09375
- cotangent: bfloat16 [4096, 4096], P(('seq', 'tp')), may hold values from -6 to 6
Outputs:
- block_out: bfloat16 [4096, 4096], P(('seq', 'tp'))
- query_grad: bfloat16 [4096, 4096], P('seq', 'tp')
- key_grad: bfloat16 [4096, 4096], P('seq', 'tp')
- value_grad: bfloat16 [4096, 4096], P('seq', 'tp')
- weight_grad: bfloat16 [4096, 4096], P('tp', 'seq')
The draws below stay inside these ranges and needn't reach their ends.
All inputs are finite; a program needn't handle non-finite values.
Results may differ from the reference program's by a relative error of at most 0.012.
Values may be sent and summed in bfloat16 or wider, within the bound.
No kernel may reach another device: no remote copies, remote signals or barrier semaphores. Data moves between devices by JAX's collectives and lax.ppermute only.
A program may use at most 128 MiB of HBM per device.

```python
import jax
import jax.numpy as jnp
from jax import lax

H = 4096
D = 4096
GROUP = 16
TAPS = 128
SHORT = 7
TOK_DEV = 512
TOKENS = 4096
N_SEQ = 8
N_TP = 4


def raised(values, stream_key, source, target, blocks, factor):
    def block_of(position):
        return (jnp.arange(values.shape[position]) // (values.shape[position] // blocks)).reshape((-1,) + (1,) * (values.ndim - 1 - position))

    near = jax.random.permutation(stream_key, blocks)[block_of(target)]
    second = (block_of(target) + blocks // 2) % blocks
    return jnp.where((block_of(source) == near) | (block_of(source) == second), factor * values, values)


def level_of(own_key, shape, shards, least, high):
    gain = 1.0
    for position, parts in shards:
        steps = jax.random.uniform(jax.random.fold_in(jax.random.fold_in(own_key, 6), position), (parts,), jnp.float32, least / len(shards), high / len(shards))
        gain = gain * jnp.repeat(jnp.exp(steps), shape[position] // parts).reshape((-1,) + (1,) * (len(shape) - 1 - position))
    return gain


def scatter_about(key, extent, deviation, most, cuts=(), held_as=jnp.bfloat16):
    gain = level_of(key, extent, cuts, -0.22, 0.18) if cuts else 1.0
    values = jax.random.normal(key, extent, jnp.float32) * deviation * gain
    return jnp.minimum(jnp.maximum(values, -most), most).astype(held_as)


def gaussian_with(key, shape, scale, most, cuts, heavy, held_as=jnp.bfloat16):
    entries = scale * jax.random.normal(key, shape, jnp.float32)
    if cuts:
        entries = entries * level_of(key, shape, cuts, -0.22, 0.18)
    return jnp.clip(raised(entries, jax.random.fold_in(key, 3), *heavy), -most, most).astype(held_as)


def setup_inputs(seed: int = 0) -> dict:
    arg_keys = jax.random.split(jax.random.key(seed), 8)
    query_in = scatter_about(arg_keys[0], (TOKENS, H), 1.0, 6.0, ((0, 8), (1, 4)))
    key_in = scatter_about(arg_keys[1], (TOKENS, H), 1.0, 6.0, ((0, 8), (1, 4)))
    value_in = scatter_about(arg_keys[2], (TOKENS, H), 1.0, 6.0, ((0, 8), (1, 4)))
    feature_taps = scatter_about(arg_keys[3], (SHORT, 3, H), SHORT ** -0.5, 2.0, ((2, 4),), jnp.float32)
    filter_taps = scatter_about(arg_keys[4], (H // GROUP, TAPS), TAPS ** -0.5, 0.5, ((0, 4),))
    out_weight = scatter_about(arg_keys[5], (H, D), H ** -0.5, 0.09375, ((0, 4),))
    cotangent = gaussian_with(arg_keys[6], (TOKENS, D), 1.0, 6.0, ((0, 32),), (0, 1, 32, 2.75))
    return {"query_in": query_in, "key_in": key_in, "value_in": value_in, "feature_taps": feature_taps, "filter_taps": filter_taps, "out_weight": out_weight, "cotangent": cotangent}


def featurize(extended, feature_taps, out_rows):
    tap_span = feature_taps.shape[0]
    summed = jnp.zeros((out_rows,) + extended.shape[1:], jnp.float32)
    for offset in range(tap_span):
        first_row = tap_span - 1 - offset
        summed = summed + feature_taps[offset] * extended[first_row:first_row + out_rows].astype(jnp.float32)
    return summed


def spread_back(extended, feature_taps, out_rows):
    tap_span = feature_taps.shape[0]
    summed = jnp.zeros((out_rows,) + extended.shape[1:], jnp.float32)
    for offset in range(tap_span):
        summed = summed + feature_taps[offset] * extended[offset:offset + out_rows]
    return summed


def causal_sum(values, filter_full):
    tap_count, channels = filter_full.shape
    row_count = values.shape[0]
    padded = jnp.concatenate([jnp.zeros((tap_count, channels), values.dtype), values], axis=0)

    def add_lag(lag_step, summed):
        lag_value = jnp.asarray(lag_step).astype(jnp.int32)
        weight_row = lax.dynamic_index_in_dim(filter_full, lag_value, 0, keepdims=False)
        shifted = lax.dynamic_slice_in_dim(padded, (tap_count - lag_value).astype(jnp.int32), row_count, 0)
        return summed + weight_row * shifted

    return lax.fori_loop(0, tap_count, add_lag, jnp.zeros_like(values))


def anti_sum(values, filter_full):
    tap_count, channels = filter_full.shape
    row_count = values.shape[0]
    padded = jnp.concatenate([values, jnp.zeros((tap_count, channels), values.dtype)], axis=0)

    def add_lag(lag_step, summed):
        lag_value = jnp.asarray(lag_step).astype(jnp.int32)
        weight_row = lax.dynamic_index_in_dim(filter_full, lag_value, 0, keepdims=False)
        shifted = lax.dynamic_slice_in_dim(padded, lag_value, row_count, 0)
        return summed + weight_row * shifted

    return lax.fori_loop(0, tap_count, add_lag, jnp.zeros_like(values))


def reference(query_in, key_in, value_in, feature_taps, filter_taps, out_weight, cotangent):
    token_count, channels = query_in.shape
    tap_span = feature_taps.shape[0]
    stacked = jnp.stack([query_in, key_in, value_in], axis=1)
    padded = jnp.concatenate([jnp.zeros((tap_span - 1, 3, channels), stacked.dtype), stacked], axis=0)
    features = featurize(padded, feature_taps, token_count)
    query_feat = features[:, 0]
    key_feat = features[:, 1]
    value_feat = features[:, 2]
    mix_rows = (key_feat * value_feat).astype(jnp.bfloat16)
    filter_full = jnp.repeat(filter_taps.astype(jnp.float32), GROUP, axis=0).T
    long_conv = causal_sum(mix_rows.astype(jnp.float32), filter_full)
    gated_rows = (query_feat * long_conv).astype(jnp.bfloat16)

    slice_width = channels // N_TP
    block_out = jnp.zeros((token_count, out_weight.shape[1]), jnp.float32)
    for member in range(N_TP):
        first_channel = member * slice_width
        local_sum = jnp.dot(gated_rows[:, first_channel:first_channel + slice_width],
                            out_weight[first_channel:first_channel + slice_width],
                            preferred_element_type=jnp.float32)
        block_out = block_out + lax.optimization_barrier(local_sum.astype(jnp.bfloat16)).astype(jnp.float32)
    block_out = block_out.astype(jnp.bfloat16)

    grad_gated = jnp.dot(cotangent, out_weight.T, preferred_element_type=jnp.float32)
    grad_conv = (grad_gated * query_feat).astype(jnp.bfloat16)
    grad_query = grad_gated * long_conv
    grad_mix = anti_sum(grad_conv.astype(jnp.float32), filter_full)
    grad_features = jnp.stack([grad_query, grad_mix * value_feat, grad_mix * key_feat], axis=1)
    padded_grad = jnp.concatenate([grad_features, jnp.zeros((tap_span - 1, 3, channels), jnp.float32)], axis=0)
    grad_inputs = spread_back(padded_grad, feature_taps, token_count).astype(jnp.bfloat16)

    grad_scale = TOKENS ** -0.5
    gated_blocks = gated_rows.reshape(N_SEQ, TOK_DEV, channels)
    cotangent_blocks = cotangent.reshape(N_SEQ, TOK_DEV, cotangent.shape[1])

    def add_shard(running, shard_pair):
        local_grad = jnp.dot(shard_pair[0].T, shard_pair[1], preferred_element_type=jnp.float32) * grad_scale
        return running + lax.optimization_barrier(local_grad.astype(jnp.bfloat16)).astype(jnp.float32), None

    weight_grad, unused = lax.scan(add_shard, jnp.zeros((channels, cotangent.shape[1]), jnp.float32),
                                   (gated_blocks, cotangent_blocks))
    return (block_out, grad_inputs[:, 0], grad_inputs[:, 1], grad_inputs[:, 2], weight_grad.astype(jnp.bfloat16))
```

```python
import jax
import jax.numpy as jnp
from jax import lax
from jax.sharding import PartitionSpec as P


def passed_along(value, axis, steps):
    count = lax.axis_size(axis)
    leading, last = (max(0, -steps), min(count, count - steps))
    return lax.ppermute(value, axis, [(source, source + steps) for source in range(leading, last)])


def featurize(extended, feature_taps, out_rows):
    tap_span = feature_taps.shape[0]
    summed = jnp.zeros((out_rows,) + extended.shape[1:], jnp.float32)
    for offset in range(tap_span):
        first_row = tap_span - 1 - offset
        summed = summed + feature_taps[offset] * extended[first_row : first_row + out_rows].astype(
            jnp.float32
        )
    return summed


def spread_back(extended, feature_taps, out_rows):
    tap_span = feature_taps.shape[0]
    summed = jnp.zeros((out_rows,) + extended.shape[1:], jnp.float32)
    for offset in range(tap_span):
        summed = summed + feature_taps[offset] * extended[offset : offset + out_rows]
    return summed


def band_table(filter_taps, reverse=False):
    tap_count = filter_taps.shape[1]
    window_rows = 2 * tap_count
    lag_index = jnp.arange(tap_count)[:, None, None]
    row_index = jnp.arange(window_rows)[None, :, None]
    col_index = jnp.arange(tap_count)[None, None, :]
    if reverse:
        select = (row_index - col_index == lag_index).astype(jnp.bfloat16)
    else:
        select = (col_index + tap_count - row_index == lag_index).astype(jnp.bfloat16)
    select = select.reshape(tap_count, window_rows * tap_count)
    toeplitz_table = jnp.dot(filter_taps, select, preferred_element_type=jnp.float32)
    return toeplitz_table.astype(jnp.bfloat16).reshape(filter_taps.shape[0], window_rows, tap_count)


def band_mix(padded_rows, toeplitz_table):
    group_count, window_rows, tap_count = toeplitz_table.shape
    row_count = padded_rows.shape[0] - tap_count
    block_count = row_count // tap_count
    channels = padded_rows.shape[1]
    lower_half = padded_rows[:row_count].reshape(block_count, tap_count, channels)
    upper_half = padded_rows[tap_count:].reshape(block_count, tap_count, channels)
    window = jnp.concatenate([lower_half, upper_half], axis=1)
    window = window.reshape(block_count, window_rows, group_count, channels // group_count)
    mixed_rows = jnp.einsum(
        "nwgc,gwt->ntgc", window, toeplitz_table, preferred_element_type=jnp.float32
    )
    return mixed_rows.reshape(row_count, channels)


def per_device(query_in, key_in, value_in, feature_taps, filter_taps, out_weight, cotangent):
    row_count, channels = query_in.shape
    tap_count = filter_taps.shape[1]
    tap_span = feature_taps.shape[0]
    stacked = jnp.stack([query_in, key_in, value_in], axis=1)
    before = passed_along(stacked[row_count - tap_span + 1 :], "seq", 1)
    features = featurize(jnp.concatenate([before, stacked], axis=0), feature_taps, row_count)
    mix_rows = (features[:, 1] * features[:, 2]).astype(jnp.bfloat16)
    mix_before = passed_along(mix_rows[row_count - tap_count :], "seq", 1)
    padded_mix = jnp.concatenate([mix_before, mix_rows], axis=0)
    query_feat = features[:, 0]
    key_feat = features[:, 1]
    value_feat = features[:, 2]
    toeplitz_rows = band_table(filter_taps)
    long_conv = band_mix(padded_mix, toeplitz_rows)
    gated_rows = (query_feat * long_conv).astype(jnp.bfloat16)
    block_out = lax.psum_scatter(
        jnp.dot(gated_rows, out_weight, preferred_element_type=jnp.float32).astype(jnp.bfloat16),
        "tp",
        scatter_dimension=0,
        tiled=True,
    )
    full_cotangent = lax.all_gather(cotangent, "tp", axis=0, tiled=True)
    grad_gated = lax.dot_general(
        full_cotangent, out_weight, (((1,), (1,)), ((), ())), preferred_element_type=jnp.float32
    )
    grad_conv = (grad_gated * query_feat).astype(jnp.bfloat16)
    grad_query = grad_gated * long_conv
    conv_after = passed_along(grad_conv[:tap_count], "seq", -1)
    grad_mix = band_mix(
        jnp.concatenate([grad_conv, conv_after], axis=0), band_table(filter_taps, reverse=True)
    )
    grad_features = jnp.stack([grad_query, grad_mix * value_feat, grad_mix * key_feat], axis=1)
    features_after = passed_along(
        grad_features[: tap_span - 1].astype(jnp.bfloat16), "seq", -1
    ).astype(jnp.float32)
    grad_inputs = spread_back(
        jnp.concatenate([grad_features, features_after], axis=0), feature_taps, row_count
    ).astype(jnp.bfloat16)
    seq_count = lax.axis_size("seq")
    grad_scale = (row_count * seq_count) ** (-0.5)
    local_grad = (
        lax.dot_general(
            gated_rows, full_cotangent, (((0,), (0,)), ((), ())), preferred_element_type=jnp.float32
        )
        * grad_scale
    )
    summed_grad = lax.psum_scatter(
        local_grad.astype(jnp.bfloat16), "seq", scatter_dimension=1, tiled=True
    )
    return (block_out, grad_inputs[:, 0], grad_inputs[:, 1], grad_inputs[:, 2], summed_grad)


def solution(mesh):
    placed = (
        P("seq", "tp"),
        P("seq", "tp"),
        P("seq", "tp"),
        P(None, None, "tp"),
        P("tp", None),
        P("tp", None),
        P(("seq", "tp"), None),
    )
    return jax.shard_map(
        per_device,
        mesh=mesh,
        in_specs=placed,
        out_specs=(
            P(("seq", "tp"), None),
            P("seq", "tp"),
            P("seq", "tp"),
            P("seq", "tp"),
            P("tp", "seq"),
        ),
        check_vma=False,
    )
```

```python
import functools

import jax
import jax.numpy as jnp
from jax import lax
from jax.sharding import PartitionSpec as P


def passed_along(value, axis, steps):
    count = lax.axis_size(axis)
    leading, last = (max(0, -steps), min(count, count - steps))
    return lax.ppermute(value, axis, [(source, source + steps) for source in range(leading, last)])


def featurize(extended, feature_taps, out_rows):
    tap_span = feature_taps.shape[0]
    summed = jnp.zeros((out_rows,) + extended.shape[1:], jnp.float32)
    for offset in range(tap_span):
        first_row = tap_span - 1 - offset
        summed = summed + feature_taps[offset] * extended[first_row : first_row + out_rows].astype(
            jnp.float32
        )
    return summed


def spread_back(extended, feature_taps, out_rows):
    tap_span = feature_taps.shape[0]
    summed = jnp.zeros((out_rows,) + extended.shape[1:], jnp.float32)
    for offset in range(tap_span):
        summed = summed + feature_taps[offset] * extended[offset : offset + out_rows]
    return summed


def band_table(filter_taps, reverse=False):
    tap_count = filter_taps.shape[1]
    window_rows = 2 * tap_count
    lag_index = jnp.arange(tap_count)[:, None, None]
    row_index = jnp.arange(window_rows)[None, :, None]
    col_index = jnp.arange(tap_count)[None, None, :]
    if reverse:
        select = (row_index - col_index == lag_index).astype(jnp.bfloat16)
    else:
        select = (col_index + tap_count - row_index == lag_index).astype(jnp.bfloat16)
    select = select.reshape(tap_count, window_rows * tap_count)
    toeplitz_table = jnp.dot(filter_taps, select, preferred_element_type=jnp.float32)
    return toeplitz_table.astype(jnp.bfloat16).reshape(filter_taps.shape[0], window_rows, tap_count)


def band_mix(padded_rows, toeplitz_table):
    group_count, window_rows, tap_count = toeplitz_table.shape
    row_count = padded_rows.shape[0] - tap_count
    block_count = row_count // tap_count
    channels = padded_rows.shape[1]
    lower_half = padded_rows[:row_count].reshape(block_count, tap_count, channels)
    upper_half = padded_rows[tap_count:].reshape(block_count, tap_count, channels)
    window = jnp.concatenate([lower_half, upper_half], axis=1)
    window = window.reshape(block_count, window_rows, group_count, channels // group_count)
    mixed_rows = jnp.einsum(
        "nwgc,gwt->ntgc", window, toeplitz_table, preferred_element_type=jnp.float32
    )
    return mixed_rows.reshape(row_count, channels)


def per_device(query_in, key_in, value_in, feature_taps, filter_taps, out_weight, cotangent, ring):
    row_count, channels = query_in.shape
    tap_count = filter_taps.shape[1]
    tap_span = feature_taps.shape[0]
    stacked = jnp.stack([query_in, key_in, value_in], axis=1)
    before = passed_along(stacked[row_count - tap_span + 1 :], "seq", 1)
    features = featurize(jnp.concatenate([before, stacked], axis=0), feature_taps, row_count)
    mix_rows = (features[:, 1] * features[:, 2]).astype(jnp.bfloat16)
    mix_before = passed_along(mix_rows[row_count - tap_count :], "seq", 1)
    padded_mix = jnp.concatenate([mix_before, mix_rows], axis=0)
    query_feat = features[:, 0]
    key_feat = features[:, 1]
    value_feat = features[:, 2]
    toeplitz_rows = band_table(filter_taps)
    long_conv = band_mix(padded_mix, toeplitz_rows)
    gated_rows = (query_feat * long_conv).astype(jnp.bfloat16)
    block_out = lax.psum_scatter(
        jnp.dot(gated_rows, out_weight, preferred_element_type=jnp.float32).astype(jnp.bfloat16),
        "tp",
        scatter_dimension=0,
        tiled=True,
    )
    full_cotangent = lax.all_gather(cotangent, "tp", axis=0, tiled=True)
    grad_gated = lax.dot_general(
        full_cotangent, out_weight, (((1,), (1,)), ((), ())), preferred_element_type=jnp.float32
    )
    grad_conv = (grad_gated * query_feat).astype(jnp.bfloat16)
    grad_query = grad_gated * long_conv
    conv_after = passed_along(grad_conv[:tap_count], "seq", -1)
    grad_mix = band_mix(
        jnp.concatenate([grad_conv, conv_after], axis=0), band_table(filter_taps, reverse=True)
    )
    grad_features = jnp.stack([grad_query, grad_mix * value_feat, grad_mix * key_feat], axis=1)
    features_after = passed_along(
        grad_features[: tap_span - 1].astype(jnp.bfloat16), "seq", -1
    ).astype(jnp.float32)
    grad_inputs = spread_back(
        jnp.concatenate([grad_features, features_after], axis=0), feature_taps, row_count
    ).astype(jnp.bfloat16)
    seq_count = lax.axis_size("seq")
    grad_scale = (row_count * seq_count) ** (-0.5)
    summed_grad = ring_reduce_scatter(gated_rows, full_cotangent, grad_scale, ring)
    return (block_out, grad_inputs[:, 0], grad_inputs[:, 1], grad_inputs[:, 2], summed_grad)


def ring_reduce_scatter(gated_rows, full_cotangent, grad_scale, ring):
    count = len(ring)
    width = full_cotangent.shape[1] // count
    half = width // 2
    place_of = [0] * count
    for place, member in enumerate(ring):
        place_of[member] = place
    place = jnp.asarray(place_of, jnp.int32)[lax.axis_index("seq")]
    members = jnp.asarray(ring, jnp.int32)
    forward = [(ring[i], ring[(i + 1) % count]) for i in range(count)]
    backward = [(ring[(i + 1) % count], ring[i]) for i in range(count)]

    def contribution(step, direction):
        owner = members[(place - direction * (1 + step)) % count]
        first = owner * width + (0 if direction == 1 else half)
        columns = lax.dynamic_slice_in_dim(full_cotangent, first, half, 1)
        return (
            lax.dot_general(
                gated_rows, columns, (((0,), (0,)), ((), ())), preferred_element_type=jnp.float32
            )
            * grad_scale
        )

    ahead = contribution(0, 1)
    behind = contribution(0, -1)
    for step in range(1, count):
        ahead = lax.ppermute(ahead.astype(jnp.bfloat16), "seq", forward).astype(jnp.float32)
        behind = lax.ppermute(behind.astype(jnp.bfloat16), "seq", backward).astype(jnp.float32)
        ahead = ahead + contribution(step, 1)
        behind = behind + contribution(step, -1)
    return jnp.concatenate([ahead, behind], axis=1).astype(jnp.bfloat16)


def ring_order(mesh):
    axis = mesh.axis_names.index("seq")
    members = jnp.moveaxis(jnp.arange(mesh.devices.size).reshape(mesh.devices.shape), axis, 0)
    devices = mesh.devices.reshape(-1)
    column = [devices[int(i)] for i in members[:, 0].reshape(-1)]
    count = len(column)
    try:
        coords = [tuple(d.coords) + (d.core_on_chip,) for d in column]
    except AttributeError:
        return list(range(count))
    varying = [k for k in range(len(coords[0])) if len({c[k] for c in coords}) > 1]
    if len(varying) != 2:
        return list(range(count))
    sizes = [len({c[k] for c in coords}) for k in varying]
    if 2 not in sizes or sizes[0] * sizes[1] != count:
        return list(range(count))
    short, long = (varying[0], varying[1]) if sizes[0] == 2 else (varying[1], varying[0])
    low_short = min(c[short] for c in coords)
    lanes = [[], []]
    for index, c in enumerate(coords):
        lanes[0 if c[short] == low_short else 1].append((c[long], index))
    return [i for _, i in sorted(lanes[0])] + [i for _, i in sorted(lanes[1], reverse=True)]


def solution(mesh):
    placed = (
        P("seq", "tp"),
        P("seq", "tp"),
        P("seq", "tp"),
        P(None, None, "tp"),
        P("tp", None),
        P("tp", None),
        P(("seq", "tp"), None),
    )
    ring = ring_order(mesh)
    return jax.shard_map(
        functools.partial(per_device, ring=ring),
        mesh=mesh,
        in_specs=placed,
        out_specs=(
            P(("seq", "tp"), None),
            P("seq", "tp"),
            P("seq", "tp"),
            P("seq", "tp"),
            P("tp", "seq"),
        ),
        check_vma=False,
    )
```

```python
import functools

import jax
import jax.numpy as jnp
from jax import lax
from jax.sharding import PartitionSpec as P


def passed_along(value, axis, steps):
    count = lax.axis_size(axis)
    leading, last = (max(0, -steps), min(count, count - steps))
    return lax.ppermute(value, axis, [(source, source + steps) for source in range(leading, last)])


def featurize(extended, feature_taps, out_rows):
    tap_span = feature_taps.shape[0]
    summed = jnp.zeros((out_rows,) + extended.shape[1:], jnp.float32)
    for offset in range(tap_span):
        first_row = tap_span - 1 - offset
        summed = summed + feature_taps[offset] * extended[first_row : first_row + out_rows].astype(
            jnp.float32
        )
    return summed


def spread_back(extended, feature_taps, out_rows):
    tap_span = feature_taps.shape[0]
    summed = jnp.zeros((out_rows,) + extended.shape[1:], jnp.float32)
    for offset in range(tap_span):
        summed = summed + feature_taps[offset] * extended[offset : offset + out_rows]
    return summed


def band_table(filter_taps, reverse=False):
    tap_count = filter_taps.shape[1]
    window_rows = 2 * tap_count
    lag_index = jnp.arange(tap_count)[:, None, None]
    row_index = jnp.arange(window_rows)[None, :, None]
    col_index = jnp.arange(tap_count)[None, None, :]
    if reverse:
        select = (row_index - col_index == lag_index).astype(jnp.bfloat16)
    else:
        select = (col_index + tap_count - row_index == lag_index).astype(jnp.bfloat16)
    select = select.reshape(tap_count, window_rows * tap_count)
    toeplitz_table = jnp.dot(filter_taps, select, preferred_element_type=jnp.float32)
    return toeplitz_table.astype(jnp.bfloat16).reshape(filter_taps.shape[0], window_rows, tap_count)


def band_mix(padded_rows, toeplitz_table):
    group_count, window_rows, tap_count = toeplitz_table.shape
    row_count = padded_rows.shape[0] - tap_count
    block_count = row_count // tap_count
    channels = padded_rows.shape[1]
    members = channels // group_count
    by_channel = padded_rows.T
    lower_half = by_channel[:, :row_count].reshape(group_count, members * block_count, tap_count)
    upper_half = by_channel[:, tap_count:].reshape(group_count, members * block_count, tap_count)
    mixed = jnp.einsum(
        "gmw,gwt->gmt", lower_half, toeplitz_table[:, :tap_count], preferred_element_type=jnp.float32
    ) + jnp.einsum(
        "gmw,gwt->gmt", upper_half, toeplitz_table[:, tap_count:], preferred_element_type=jnp.float32
    )
    mixed = mixed.reshape(group_count, members, block_count, tap_count)
    return mixed.transpose(2, 3, 0, 1).reshape(row_count, channels)


def per_device(query_in, key_in, value_in, feature_taps, filter_taps, out_weight, cotangent, ring):
    row_count, channels = query_in.shape
    tap_count = filter_taps.shape[1]
    tap_span = feature_taps.shape[0]
    inputs = (query_in, key_in, value_in)
    before = passed_along(
        jnp.stack([rows[row_count - tap_span + 1 :] for rows in inputs], axis=0), "seq", 1
    )
    query_feat, key_feat, value_feat = (
        featurize(jnp.concatenate([before[i], inputs[i]], axis=0), feature_taps[:, i], row_count)
        for i in range(3)
    )
    mix_rows = (key_feat * value_feat).astype(jnp.bfloat16)
    mix_before = passed_along(mix_rows[row_count - tap_count :], "seq", 1)
    padded_mix = jnp.concatenate([mix_before, mix_rows], axis=0)
    toeplitz_rows = band_table(filter_taps)
    long_conv = band_mix(padded_mix, toeplitz_rows)
    gated_rows = (query_feat * long_conv).astype(jnp.bfloat16)
    block_out = lax.psum_scatter(
        jnp.dot(gated_rows, out_weight, preferred_element_type=jnp.float32).astype(jnp.bfloat16),
        "tp",
        scatter_dimension=0,
        tiled=True,
    )
    full_cotangent = lax.all_gather(cotangent, "tp", axis=0, tiled=True)
    seq_count = lax.axis_size("seq")
    grad_scale = (row_count * seq_count) ** (-0.5)
    summed_grad = ring_reduce_scatter(gated_rows, full_cotangent, grad_scale, ring)
    grad_gated = lax.dot_general(
        full_cotangent, out_weight, (((1,), (1,)), ((), ())), preferred_element_type=jnp.float32
    )
    grad_conv = (grad_gated * query_feat).astype(jnp.bfloat16)
    grad_query = grad_gated * long_conv
    conv_after = passed_along(grad_conv[:tap_count], "seq", -1)
    grad_mix = band_mix(
        jnp.concatenate([grad_conv, conv_after], axis=0), band_table(filter_taps, reverse=True)
    )
    grad_features = (grad_query, grad_mix * value_feat, grad_mix * key_feat)
    features_after = passed_along(
        jnp.stack([rows[: tap_span - 1] for rows in grad_features], axis=0).astype(jnp.bfloat16),
        "seq",
        -1,
    ).astype(jnp.float32)
    query_grad, key_grad, value_grad = (
        spread_back(
            jnp.concatenate([grad_features[i], features_after[i]], axis=0),
            feature_taps[:, i],
            row_count,
        ).astype(jnp.bfloat16)
        for i in range(3)
    )
    return (block_out, query_grad, key_grad, value_grad, summed_grad)


def ring_reduce_scatter(gated_rows, full_cotangent, grad_scale, ring):
    count = len(ring)
    width = full_cotangent.shape[1] // count
    half = width // 2
    place_of = [0] * count
    for place, member in enumerate(ring):
        place_of[member] = place
    place = jnp.asarray(place_of, jnp.int32)[lax.axis_index("seq")]
    members = jnp.asarray(ring, jnp.int32)
    forward = [(ring[i], ring[(i + 1) % count]) for i in range(count)]
    backward = [(ring[(i + 1) % count], ring[i]) for i in range(count)]

    local_grad = (
        lax.dot_general(
            gated_rows, full_cotangent, (((0,), (0,)), ((), ())), preferred_element_type=jnp.float32
        )
        * grad_scale
    )

    def contribution(step, direction):
        owner = members[(place - direction * (1 + step)) % count]
        first = owner * width + (0 if direction == 1 else half)
        return lax.dynamic_slice_in_dim(local_grad, first, half, 1)

    ahead = contribution(0, 1)
    behind = contribution(0, -1)
    for step in range(1, count):
        ahead = lax.ppermute(ahead.astype(jnp.bfloat16), "seq", forward).astype(jnp.float32)
        behind = lax.ppermute(behind.astype(jnp.bfloat16), "seq", backward).astype(jnp.float32)
        ahead = ahead + contribution(step, 1)
        behind = behind + contribution(step, -1)
    return jnp.concatenate([ahead, behind], axis=1).astype(jnp.bfloat16)


def ring_order(mesh):
    axis = mesh.axis_names.index("seq")
    members = jnp.moveaxis(jnp.arange(mesh.devices.size).reshape(mesh.devices.shape), axis, 0)
    devices = mesh.devices.reshape(-1)
    column = [devices[int(i)] for i in members[:, 0].reshape(-1)]
    count = len(column)
    try:
        coords = [tuple(d.coords) + (d.core_on_chip,) for d in column]
    except AttributeError:
        return list(range(count))
    varying = [k for k in range(len(coords[0])) if len({c[k] for c in coords}) > 1]
    if len(varying) != 2:
        return list(range(count))
    sizes = [len({c[k] for c in coords}) for k in varying]
    if 2 not in sizes or sizes[0] * sizes[1] != count:
        return list(range(count))
    short, long = (varying[0], varying[1]) if sizes[0] == 2 else (varying[1], varying[0])
    low_short = min(c[short] for c in coords)
    lanes = [[], []]
    for index, c in enumerate(coords):
        lanes[0 if c[short] == low_short else 1].append((c[long], index))
    return [i for _, i in sorted(lanes[0])] + [i for _, i in sorted(lanes[1], reverse=True)]


def solution(mesh):
    placed = (
        P("seq", "tp"),
        P("seq", "tp"),
        P("seq", "tp"),
        P(None, None, "tp"),
        P("tp", None),
        P("tp", None),
        P(("seq", "tp"), None),
    )
    ring = ring_order(mesh)
    return jax.shard_map(
        functools.partial(per_device, ring=ring),
        mesh=mesh,
        in_specs=placed,
        out_specs=(
            P(("seq", "tp"), None),
            P("seq", "tp"),
            P("seq", "tp"),
            P("seq", "tp"),
            P("tp", "seq"),
        ),
        check_vma=False,
    )
```

```python
import functools

import jax
import jax.numpy as jnp
from jax import lax
from jax.sharding import PartitionSpec as P


def passed_along(value, axis, steps):
    count = lax.axis_size(axis)
    leading, last = (max(0, -steps), min(count, count - steps))
    return lax.ppermute(value, axis, [(source, source + steps) for source in range(leading, last)])


def featurize(extended, feature_taps, out_rows):
    tap_span = feature_taps.shape[0]
    summed = jnp.zeros((out_rows,) + extended.shape[1:], jnp.float32)
    for offset in range(tap_span):
        first_row = tap_span - 1 - offset
        summed = summed + feature_taps[offset] * extended[first_row : first_row + out_rows].astype(
            jnp.float32
        )
    return summed


def spread_back(extended, feature_taps, out_rows):
    tap_span = feature_taps.shape[0]
    summed = jnp.zeros((out_rows,) + extended.shape[1:], jnp.float32)
    for offset in range(tap_span):
        summed = summed + feature_taps[offset] * extended[offset : offset + out_rows]
    return summed


def band_table(filter_taps, reverse=False):
    tap_count = filter_taps.shape[1]
    window_rows = 2 * tap_count
    lag_index = jnp.arange(tap_count)[:, None, None]
    row_index = jnp.arange(window_rows)[None, :, None]
    col_index = jnp.arange(tap_count)[None, None, :]
    if reverse:
        select = (row_index - col_index == lag_index).astype(jnp.bfloat16)
    else:
        select = (col_index + tap_count - row_index == lag_index).astype(jnp.bfloat16)
    select = select.reshape(tap_count, window_rows * tap_count)
    toeplitz_table = jnp.dot(filter_taps, select, preferred_element_type=jnp.float32)
    return toeplitz_table.astype(jnp.bfloat16).reshape(filter_taps.shape[0], window_rows, tap_count)


def band_mix(padded_rows, toeplitz_table):
    group_count, window_rows, tap_count = toeplitz_table.shape
    row_count = padded_rows.shape[0] - tap_count
    block_count = row_count // tap_count
    channels = padded_rows.shape[1]
    members = channels // group_count
    by_channel = padded_rows.T
    lower_half = by_channel[:, :row_count].reshape(group_count, members * block_count, tap_count)
    upper_half = by_channel[:, tap_count:].reshape(group_count, members * block_count, tap_count)
    mixed = jnp.einsum(
        "gmw,gwt->gmt", lower_half, toeplitz_table[:, :tap_count], preferred_element_type=jnp.float32
    ) + jnp.einsum(
        "gmw,gwt->gmt", upper_half, toeplitz_table[:, tap_count:], preferred_element_type=jnp.float32
    )
    mixed = mixed.reshape(group_count, members, block_count, tap_count)
    return mixed.transpose(2, 3, 0, 1).reshape(row_count, channels)


def per_device(query_in, key_in, value_in, feature_taps, filter_taps, out_weight, cotangent, ring):
    row_count, channels = query_in.shape
    tap_count = filter_taps.shape[1]
    tap_span = feature_taps.shape[0]
    full_cotangent = lax.all_gather(cotangent, "tp", axis=0, tiled=True)
    inputs = (query_in, key_in, value_in)
    before = passed_along(
        jnp.stack([rows[row_count - tap_span + 1 :] for rows in inputs], axis=0), "seq", 1
    )
    query_feat, key_feat, value_feat = (
        featurize(jnp.concatenate([before[i], inputs[i]], axis=0), feature_taps[:, i], row_count)
        for i in range(3)
    )
    mix_rows = (key_feat * value_feat).astype(jnp.bfloat16)
    mix_before = passed_along(mix_rows[row_count - tap_count :], "seq", 1)
    padded_mix = jnp.concatenate([mix_before, mix_rows], axis=0)
    long_conv = band_mix(padded_mix, band_table(filter_taps))
    gated_rows = (query_feat * long_conv).astype(jnp.bfloat16)
    seq_count = lax.axis_size("seq")
    grad_scale = (row_count * seq_count) ** (-0.5)

    def project(state):
        gated_rows, out_weight = state
        block_out = lax.psum_scatter(
            jnp.dot(gated_rows, out_weight, preferred_element_type=jnp.float32).astype(jnp.bfloat16),
            "tp",
            scatter_dimension=0,
            tiled=True,
        )
        return (block_out, out_weight)

    def gate_back(state):
        block_out, out_weight = state
        grad_gated = lax.dot_general(
            full_cotangent, out_weight, (((1,), (1,)), ((), ())), preferred_element_type=jnp.float32
        )
        grad_conv = (grad_gated * query_feat).astype(jnp.bfloat16)
        grad_query = grad_gated * long_conv
        conv_after = passed_along(grad_conv[:tap_count], "seq", -1)
        return (block_out, grad_conv, conv_after, grad_query)

    def filter_back(state):
        block_out, grad_conv, conv_after, grad_query = state
        grad_mix = band_mix(
            jnp.concatenate([grad_conv, conv_after], axis=0), band_table(filter_taps, reverse=True)
        )
        grad_features = (grad_query, grad_mix * value_feat, grad_mix * key_feat)
        features_after = passed_along(
            jnp.stack([rows[: tap_span - 1] for rows in grad_features], axis=0).astype(jnp.bfloat16),
            "seq",
            -1,
        )
        return (block_out, grad_features, features_after)

    def feature_back(state):
        block_out, grad_features, features_after = state
        grads = tuple(
            spread_back(
                jnp.concatenate([grad_features[i], features_after[i].astype(jnp.float32)], axis=0),
                feature_taps[:, i],
                row_count,
            ).astype(jnp.bfloat16)
            for i in range(3)
        )
        return (block_out,) + grads

    stages = [project, gate_back, filter_back, feature_back]
    state, summed_grad = ring_reduce_scatter(
        gated_rows, full_cotangent, grad_scale, ring, stages, (gated_rows, out_weight)
    )
    return state + (summed_grad,)


def ring_reduce_scatter(gated_rows, full_cotangent, grad_scale, ring, stages, state):
    count = len(ring)
    width = full_cotangent.shape[1] // count
    half = width // 2
    place_of = [0] * count
    for place, member in enumerate(ring):
        place_of[member] = place
    place = jnp.asarray(place_of, jnp.int32)[lax.axis_index("seq")]
    members = jnp.asarray(ring, jnp.int32)
    forward = [(ring[i], ring[(i + 1) % count]) for i in range(count)]
    backward = [(ring[(i + 1) % count], ring[i]) for i in range(count)]
    blocks = full_cotangent.reshape(full_cotangent.shape[0], count, 2, half).transpose(1, 2, 0, 3)
    local_grad = (
        jnp.einsum("tc,bhtd->bhcd", gated_rows, blocks, preferred_element_type=jnp.float32)
        * grad_scale
    )

    def contribution(step, direction):
        owner = members[(place - direction * (1 + step)) % count]
        block = lax.dynamic_index_in_dim(local_grad, owner, 0, keepdims=False)
        return block[0 if direction == 1 else 1]

    ahead = contribution(0, 1)
    behind = contribution(0, -1)
    stages = list(stages)
    for step in range(1, count):
        sent_ahead = ahead.astype(jnp.bfloat16)
        sent_behind = behind.astype(jnp.bfloat16)
        if stages:
            sent_ahead, sent_behind, state = lax.optimization_barrier(
                (sent_ahead, sent_behind, state)
            )
        ahead = lax.ppermute(sent_ahead, "seq", forward).astype(jnp.float32)
        behind = lax.ppermute(sent_behind, "seq", backward).astype(jnp.float32)
        if stages:
            state = stages.pop(0)(state)
        ahead = ahead + contribution(step, 1)
        behind = behind + contribution(step, -1)
    while stages:
        state = stages.pop(0)(state)
    return state, jnp.concatenate([ahead, behind], axis=1).astype(jnp.bfloat16)


def ring_order(mesh):
    axis = mesh.axis_names.index("seq")
    members = jnp.moveaxis(jnp.arange(mesh.devices.size).reshape(mesh.devices.shape), axis, 0)
    devices = mesh.devices.reshape(-1)
    column = [devices[int(i)] for i in members[:, 0].reshape(-1)]
    count = len(column)
    try:
        coords = [tuple(d.coords) + (d.core_on_chip,) for d in column]
    except AttributeError:
        return list(range(count))
    varying = [k for k in range(len(coords[0])) if len({c[k] for c in coords}) > 1]
    if len(varying) != 2:
        return list(range(count))
    sizes = [len({c[k] for c in coords}) for k in varying]
    if 2 not in sizes or sizes[0] * sizes[1] != count:
        return list(range(count))
    short, long = (varying[0], varying[1]) if sizes[0] == 2 else (varying[1], varying[0])
    low_short = min(c[short] for c in coords)
    lanes = [[], []]
    for index, c in enumerate(coords):
        lanes[0 if c[short] == low_short else 1].append((c[long], index))
    return [i for _, i in sorted(lanes[0])] + [i for _, i in sorted(lanes[1], reverse=True)]


def solution(mesh):
    placed = (
        P("seq", "tp"),
        P("seq", "tp"),
        P("seq", "tp"),
        P(None, None, "tp"),
        P("tp", None),
        P("tp", None),
        P(("seq", "tp"), None),
    )
    ring = ring_order(mesh)
    return jax.shard_map(
        functools.partial(per_device, ring=ring),
        mesh=mesh,
        in_specs=placed,
        out_specs=(
            P(("seq", "tp"), None),
            P("seq", "tp"),
            P("seq", "tp"),
            P("seq", "tp"),
            P("tp", "seq"),
        ),
        check_vma=False,
    )
```

```python
import functools

import jax
import jax.numpy as jnp
from jax import lax
from jax.sharding import PartitionSpec as P


def passed_along(value, axis, steps):
    count = lax.axis_size(axis)
    leading, last = (max(0, -steps), min(count, count - steps))
    return lax.ppermute(value, axis, [(source, source + steps) for source in range(leading, last)])


def featurize(extended, feature_taps, out_rows):
    tap_span = feature_taps.shape[0]
    summed = jnp.zeros((out_rows,) + extended.shape[1:], jnp.float32)
    for offset in range(tap_span):
        first_row = tap_span - 1 - offset
        summed = summed + feature_taps[offset] * extended[first_row : first_row + out_rows].astype(
            jnp.float32
        )
    return summed


def spread_back(extended, feature_taps, out_rows):
    tap_span = feature_taps.shape[0]
    summed = jnp.zeros((out_rows,) + extended.shape[1:], jnp.float32)
    for offset in range(tap_span):
        summed = summed + feature_taps[offset] * extended[offset : offset + out_rows]
    return summed


def band_table(filter_taps, reverse=False):
    tap_count = filter_taps.shape[1]
    window_rows = 2 * tap_count
    lag_index = jnp.arange(tap_count)[:, None, None]
    row_index = jnp.arange(window_rows)[None, :, None]
    col_index = jnp.arange(tap_count)[None, None, :]
    if reverse:
        select = (row_index - col_index == lag_index).astype(jnp.bfloat16)
    else:
        select = (col_index + tap_count - row_index == lag_index).astype(jnp.bfloat16)
    select = select.reshape(tap_count, window_rows * tap_count)
    toeplitz_table = jnp.dot(filter_taps, select, preferred_element_type=jnp.float32)
    return toeplitz_table.astype(jnp.bfloat16).reshape(filter_taps.shape[0], window_rows, tap_count)


def band_mix(padded_rows, toeplitz_table):
    group_count, window_rows, tap_count = toeplitz_table.shape
    row_count = padded_rows.shape[0] - tap_count
    block_count = row_count // tap_count
    channels = padded_rows.shape[1]
    members = channels // group_count
    by_channel = padded_rows.T
    lower_half = by_channel[:, :row_count].reshape(group_count, members * block_count, tap_count)
    upper_half = by_channel[:, tap_count:].reshape(group_count, members * block_count, tap_count)
    mixed = jnp.einsum(
        "gmw,gwt->gmt", lower_half, toeplitz_table[:, :tap_count], preferred_element_type=jnp.float32
    ) + jnp.einsum(
        "gmw,gwt->gmt", upper_half, toeplitz_table[:, tap_count:], preferred_element_type=jnp.float32
    )
    mixed = mixed.reshape(group_count, members, block_count, tap_count)
    return mixed.transpose(2, 3, 0, 1).reshape(row_count, channels)


def per_device(query_in, key_in, value_in, feature_taps, filter_taps, out_weight, cotangent, ring):
    row_count, channels = query_in.shape
    tap_count = filter_taps.shape[1]
    tap_span = feature_taps.shape[0]
    full_cotangent = lax.all_gather(cotangent, "tp", axis=0, tiled=True)
    inputs = (query_in, key_in, value_in)
    before = passed_along(
        jnp.stack([rows[row_count - tap_span + 1 :] for rows in inputs], axis=0), "seq", 1
    )
    query_feat, key_feat, value_feat = (
        featurize(jnp.concatenate([before[i], inputs[i]], axis=0), feature_taps[:, i], row_count)
        for i in range(3)
    )
    mix_rows = (key_feat * value_feat).astype(jnp.bfloat16)
    mix_before = passed_along(mix_rows[row_count - tap_count :], "seq", 1)
    padded_mix = jnp.concatenate([mix_before, mix_rows], axis=0)
    long_conv = band_mix(padded_mix, band_table(filter_taps))
    gated_rows = (query_feat * long_conv).astype(jnp.bfloat16)
    seq_count = lax.axis_size("seq")
    grad_scale = (row_count * seq_count) ** (-0.5)

    def project(state):
        gated_rows, out_weight = state
        block_out = lax.psum_scatter(
            jnp.dot(gated_rows, out_weight, preferred_element_type=jnp.float32).astype(jnp.bfloat16),
            "tp",
            scatter_dimension=0,
            tiled=True,
        )
        return (block_out, out_weight)

    def gate_back(state):
        block_out, out_weight = state
        grad_gated = lax.dot_general(
            full_cotangent, out_weight, (((1,), (1,)), ((), ())), preferred_element_type=jnp.float32
        )
        grad_conv = (grad_gated * query_feat).astype(jnp.bfloat16)
        grad_query = grad_gated * long_conv
        conv_after = passed_along(grad_conv[:tap_count], "seq", -1)
        return (block_out, grad_conv, conv_after, grad_query)

    def filter_back(state):
        block_out, grad_conv, conv_after, grad_query = state
        grad_mix = band_mix(
            jnp.concatenate([grad_conv, conv_after], axis=0), band_table(filter_taps, reverse=True)
        )
        grad_features = (grad_query, grad_mix * value_feat, grad_mix * key_feat)
        features_after = passed_along(
            jnp.stack([rows[: tap_span - 1] for rows in grad_features], axis=0).astype(jnp.bfloat16),
            "seq",
            -1,
        )
        return (block_out, grad_features, features_after)

    def feature_back(state):
        block_out, grad_features, features_after = state
        grads = tuple(
            spread_back(
                jnp.concatenate([grad_features[i], features_after[i].astype(jnp.float32)], axis=0),
                feature_taps[:, i],
                row_count,
            ).astype(jnp.bfloat16)
            for i in range(3)
        )
        return (block_out,) + grads

    stages = [project, gate_back, filter_back, feature_back]
    state, summed_grad = ring_reduce_scatter(
        gated_rows, full_cotangent, grad_scale, ring, stages, (gated_rows, out_weight)
    )
    return state + (summed_grad,)


def ring_reduce_scatter(gated_rows, full_cotangent, grad_scale, ring, stages, state):
    count = len(ring)
    width = full_cotangent.shape[1] // count
    half = width // 2
    place_of = [0] * count
    for place, member in enumerate(ring):
        place_of[member] = place
    place = jnp.asarray(place_of, jnp.int32)[lax.axis_index("seq")]
    members = jnp.asarray(ring, jnp.int32)
    forward = [(ring[i], ring[(i + 1) % count]) for i in range(count)]
    backward = [(ring[(i + 1) % count], ring[i]) for i in range(count)]
    local_grad = (
        lax.dot_general(
            gated_rows, full_cotangent, (((0,), (0,)), ((), ())), preferred_element_type=jnp.float32
        )
        * grad_scale
    )

    def contribution(step, direction):
        owner = members[(place - direction * (1 + step)) % count]
        first = owner * width + (0 if direction == 1 else half)
        return lax.dynamic_slice_in_dim(local_grad, first, half, 1)

    ahead = contribution(0, 1)
    behind = contribution(0, -1)
    stages = list(stages)
    for step in range(1, count):
        sent_ahead = ahead.astype(jnp.bfloat16)
        sent_behind = behind.astype(jnp.bfloat16)
        if stages:
            sent_ahead, sent_behind, state = lax.optimization_barrier(
                (sent_ahead, sent_behind, state)
            )
        ahead = lax.ppermute(sent_ahead, "seq", forward)
        behind = lax.ppermute(sent_behind, "seq", backward)
        if stages:
            state = stages.pop(0)(state)
            ahead, behind, state = lax.optimization_barrier((ahead, behind, state))
        ahead = ahead.astype(jnp.float32) + contribution(step, 1)
        behind = behind.astype(jnp.float32) + contribution(step, -1)
    while stages:
        state = stages.pop(0)(state)
    return state, jnp.concatenate([ahead, behind], axis=1).astype(jnp.bfloat16)


def ring_order(mesh):
    axis = mesh.axis_names.index("seq")
    members = jnp.moveaxis(jnp.arange(mesh.devices.size).reshape(mesh.devices.shape), axis, 0)
    devices = mesh.devices.reshape(-1)
    column = [devices[int(i)] for i in members[:, 0].reshape(-1)]
    count = len(column)
    try:
        coords = [tuple(d.coords) + (d.core_on_chip,) for d in column]
    except AttributeError:
        return list(range(count))
    varying = [k for k in range(len(coords[0])) if len({c[k] for c in coords}) > 1]
    if len(varying) != 2:
        return list(range(count))
    sizes = [len({c[k] for c in coords}) for k in varying]
    if 2 not in sizes or sizes[0] * sizes[1] != count:
        return list(range(count))
    short, long = (varying[0], varying[1]) if sizes[0] == 2 else (varying[1], varying[0])
    low_short = min(c[short] for c in coords)
    lanes = [[], []]
    for index, c in enumerate(coords):
        lanes[0 if c[short] == low_short else 1].append((c[long], index))
    return [i for _, i in sorted(lanes[0])] + [i for _, i in sorted(lanes[1], reverse=True)]


def solution(mesh):
    placed = (
        P("seq", "tp"),
        P("seq", "tp"),
        P("seq", "tp"),
        P(None, None, "tp"),
        P("tp", None),
        P("tp", None),
        P(("seq", "tp"), None),
    )
    ring = ring_order(mesh)
    return jax.shard_map(
        functools.partial(per_device, ring=ring),
        mesh=mesh,
        in_specs=placed,
        out_specs=(
            P(("seq", "tp"), None),
            P("seq", "tp"),
            P("seq", "tp"),
            P("seq", "tp"),
            P("tp", "seq"),
        ),
        check_vma=False,
    )
```

```python
import functools

import jax
import jax.numpy as jnp
from jax import lax
from jax.sharding import PartitionSpec as P


def passed_along(value, axis, steps):
    count = lax.axis_size(axis)
    leading, last = (max(0, -steps), min(count, count - steps))
    return lax.ppermute(value, axis, [(source, source + steps) for source in range(leading, last)])


def featurize(extended, feature_taps, out_rows):
    tap_span = feature_taps.shape[0]
    summed = jnp.zeros((out_rows,) + extended.shape[1:], jnp.float32)
    for offset in range(tap_span):
        first_row = tap_span - 1 - offset
        summed = summed + feature_taps[offset] * extended[first_row : first_row + out_rows].astype(
            jnp.float32
        )
    return summed


def spread_back(extended, feature_taps, out_rows):
    tap_span = feature_taps.shape[0]
    summed = jnp.zeros((out_rows,) + extended.shape[1:], jnp.float32)
    for offset in range(tap_span):
        summed = summed + feature_taps[offset] * extended[offset : offset + out_rows]
    return summed


def band_table(filter_taps, reverse=False):
    tap_count = filter_taps.shape[1]
    window_rows = 2 * tap_count
    lag_index = jnp.arange(tap_count)[:, None, None]
    row_index = jnp.arange(window_rows)[None, :, None]
    col_index = jnp.arange(tap_count)[None, None, :]
    if reverse:
        select = (row_index - col_index == lag_index).astype(jnp.bfloat16)
    else:
        select = (col_index + tap_count - row_index == lag_index).astype(jnp.bfloat16)
    select = select.reshape(tap_count, window_rows * tap_count)
    toeplitz_table = jnp.dot(filter_taps, select, preferred_element_type=jnp.float32)
    return toeplitz_table.astype(jnp.bfloat16).reshape(filter_taps.shape[0], window_rows, tap_count)


def band_mix(padded_rows, toeplitz_table):
    group_count, window_rows, tap_count = toeplitz_table.shape
    row_count = padded_rows.shape[0] - tap_count
    block_count = row_count // tap_count
    channels = padded_rows.shape[1]
    members = channels // group_count
    by_channel = padded_rows.T
    lower_half = by_channel[:, :row_count].reshape(group_count, members * block_count, tap_count)
    upper_half = by_channel[:, tap_count:].reshape(group_count, members * block_count, tap_count)
    mixed = jnp.einsum(
        "gmw,gwt->gmt", lower_half, toeplitz_table[:, :tap_count], preferred_element_type=jnp.float32
    ) + jnp.einsum(
        "gmw,gwt->gmt", upper_half, toeplitz_table[:, tap_count:], preferred_element_type=jnp.float32
    )
    mixed = mixed.reshape(group_count, members, block_count, tap_count)
    return mixed.transpose(2, 3, 0, 1).reshape(row_count, channels)


def per_device(query_in, key_in, value_in, feature_taps, filter_taps, out_weight, cotangent, ring):
    row_count, channels = query_in.shape
    tap_count = filter_taps.shape[1]
    tap_span = feature_taps.shape[0]
    full_cotangent = lax.all_gather(cotangent, "tp", axis=0, tiled=True)
    inputs = (query_in, key_in, value_in)
    before = passed_along(
        jnp.stack([rows[row_count - tap_span + 1 :] for rows in inputs], axis=0), "seq", 1
    )
    query_feat, key_feat, value_feat = (
        featurize(jnp.concatenate([before[i], inputs[i]], axis=0), feature_taps[:, i], row_count)
        for i in range(3)
    )
    mix_rows = (key_feat * value_feat).astype(jnp.bfloat16)
    mix_before = passed_along(mix_rows[row_count - tap_count :], "seq", 1)
    padded_mix = jnp.concatenate([mix_before, mix_rows], axis=0)
    long_conv = band_mix(padded_mix, band_table(filter_taps))
    gated_rows = (query_feat * long_conv).astype(jnp.bfloat16)
    seq_count = lax.axis_size("seq")
    grad_scale = (row_count * seq_count) ** (-0.5)

    projected = []

    def project(state):
        gated_rows, out_weight = state
        projected.append(
            lax.psum_scatter(
                jnp.dot(gated_rows, out_weight, preferred_element_type=jnp.float32).astype(
                    jnp.bfloat16
                ),
                "tp",
                scatter_dimension=0,
                tiled=True,
            )
        )
        return out_weight

    def gate_back(out_weight):
        grad_gated = lax.dot_general(
            full_cotangent, out_weight, (((1,), (1,)), ((), ())), preferred_element_type=jnp.float32
        )
        grad_conv = (grad_gated * query_feat).astype(jnp.bfloat16)
        grad_query = grad_gated * long_conv
        conv_after = passed_along(grad_conv[:tap_count], "seq", -1)
        return (grad_conv, conv_after, grad_query)

    def filter_back(state):
        grad_conv, conv_after, grad_query = state
        grad_mix = band_mix(
            jnp.concatenate([grad_conv, conv_after], axis=0), band_table(filter_taps, reverse=True)
        )
        grad_features = (grad_query, grad_mix * value_feat, grad_mix * key_feat)
        features_after = passed_along(
            jnp.stack([rows[: tap_span - 1] for rows in grad_features], axis=0).astype(jnp.bfloat16),
            "seq",
            -1,
        )
        return (grad_features, features_after)

    def feature_back(state):
        grad_features, features_after = state
        grads = tuple(
            spread_back(
                jnp.concatenate([grad_features[i], features_after[i].astype(jnp.float32)], axis=0),
                feature_taps[:, i],
                row_count,
            ).astype(jnp.bfloat16)
            for i in range(3)
        )
        return grads

    stages = [project, gate_back, filter_back, feature_back]
    state, summed_grad = ring_reduce_scatter(
        gated_rows, full_cotangent, grad_scale, ring, stages, (gated_rows, out_weight)
    )
    return (projected[0],) + state + (summed_grad,)


def ring_reduce_scatter(gated_rows, full_cotangent, grad_scale, ring, stages, state):
    count = len(ring)
    width = full_cotangent.shape[1] // count
    half = width // 2
    place_of = [0] * count
    for place, member in enumerate(ring):
        place_of[member] = place
    place = jnp.asarray(place_of, jnp.int32)[lax.axis_index("seq")]
    members = jnp.asarray(ring, jnp.int32)
    forward = [(ring[i], ring[(i + 1) % count]) for i in range(count)]
    backward = [(ring[(i + 1) % count], ring[i]) for i in range(count)]
    local_grad = (
        lax.dot_general(
            gated_rows, full_cotangent, (((0,), (0,)), ((), ())), preferred_element_type=jnp.float32
        )
        * grad_scale
    )

    def contribution(step, direction):
        owner = members[(place - direction * (1 + step)) % count]
        first = owner * width + (0 if direction == 1 else half)
        return lax.dynamic_slice_in_dim(local_grad, first, half, 1)

    ahead = contribution(0, 1)
    behind = contribution(0, -1)
    stages = list(stages)
    for step in range(1, count):
        sent_ahead = ahead.astype(jnp.bfloat16)
        sent_behind = behind.astype(jnp.bfloat16)
        if stages:
            sent_ahead, sent_behind, state = lax.optimization_barrier(
                (sent_ahead, sent_behind, state)
            )
        ahead = lax.ppermute(sent_ahead, "seq", forward)
        behind = lax.ppermute(sent_behind, "seq", backward)
        if stages:
            state = stages.pop(0)(state)
            ahead, behind, state = lax.optimization_barrier((ahead, behind, state))
        ahead = ahead.astype(jnp.float32) + contribution(step, 1)
        behind = behind.astype(jnp.float32) + contribution(step, -1)
    while stages:
        state = stages.pop(0)(state)
    return state, jnp.concatenate([ahead, behind], axis=1).astype(jnp.bfloat16)


def ring_order(mesh):
    axis = mesh.axis_names.index("seq")
    members = jnp.moveaxis(jnp.arange(mesh.devices.size).reshape(mesh.devices.shape), axis, 0)
    devices = mesh.devices.reshape(-1)
    column = [devices[int(i)] for i in members[:, 0].reshape(-1)]
    count = len(column)
    try:
        coords = [tuple(d.coords) + (d.core_on_chip,) for d in column]
    except AttributeError:
        return list(range(count))
    varying = [k for k in range(len(coords[0])) if len({c[k] for c in coords}) > 1]
    if len(varying) != 2:
        return list(range(count))
    sizes = [len({c[k] for c in coords}) for k in varying]
    if 2 not in sizes or sizes[0] * sizes[1] != count:
        return list(range(count))
    short, long = (varying[0], varying[1]) if sizes[0] == 2 else (varying[1], varying[0])
    low_short = min(c[short] for c in coords)
    lanes = [[], []]
    for index, c in enumerate(coords):
        lanes[0 if c[short] == low_short else 1].append((c[long], index))
    return [i for _, i in sorted(lanes[0])] + [i for _, i in sorted(lanes[1], reverse=True)]


def solution(mesh):
    placed = (
        P("seq", "tp"),
        P("seq", "tp"),
        P("seq", "tp"),
        P(None, None, "tp"),
        P("tp", None),
        P("tp", None),
        P(("seq", "tp"), None),
    )
    ring = ring_order(mesh)
    return jax.shard_map(
        functools.partial(per_device, ring=ring),
        mesh=mesh,
        in_specs=placed,
        out_specs=(
            P(("seq", "tp"), None),
            P("seq", "tp"),
            P("seq", "tp"),
            P("seq", "tp"),
            P("tp", "seq"),
        ),
        check_vma=False,
    )
```

```python
import functools

import jax
import jax.numpy as jnp
from jax import lax
from jax.experimental import pallas as pl
from jax.sharding import PartitionSpec as P


def passed_along(value, axis, steps):
    count = lax.axis_size(axis)
    leading, last = (max(0, -steps), min(count, count - steps))
    return lax.ppermute(value, axis, [(source, source + steps) for source in range(leading, last)])


def featurize(extended, feature_taps, out_rows):
    tap_span = feature_taps.shape[0]
    summed = jnp.zeros((out_rows,) + extended.shape[1:], jnp.float32)
    for offset in range(tap_span):
        first_row = tap_span - 1 - offset
        summed = summed + feature_taps[offset] * extended[first_row : first_row + out_rows].astype(
            jnp.float32
        )
    return summed


def spread_back(extended, feature_taps, out_rows):
    tap_span = feature_taps.shape[0]
    summed = jnp.zeros((out_rows,) + extended.shape[1:], jnp.float32)
    for offset in range(tap_span):
        summed = summed + feature_taps[offset] * extended[offset : offset + out_rows]
    return summed


def band_table(filter_taps, reverse=False):
    tap_count = filter_taps.shape[1]
    window_rows = 2 * tap_count
    lag_index = jnp.arange(tap_count)[:, None, None]
    out_index = jnp.arange(tap_count)[None, :, None]
    row_index = jnp.arange(window_rows)[None, None, :]
    if reverse:
        select = (row_index - out_index == lag_index).astype(jnp.bfloat16)
    else:
        select = (out_index + tap_count - row_index == lag_index).astype(jnp.bfloat16)
    select = select.reshape(tap_count, tap_count * window_rows)
    table = jnp.dot(filter_taps, select, preferred_element_type=jnp.float32)
    return table.astype(jnp.bfloat16).reshape(filter_taps.shape[0], tap_count, window_rows)


def band_mix(padded_rows, table, lane_tile=128):
    group_count, tap_count, window_rows = table.shape
    row_count = padded_rows.shape[0] - tap_count
    channels = padded_rows.shape[1]
    members = channels // group_count
    per_tile = lane_tile // members

    def body(table_ref, lower_ref, upper_ref, out_ref):
        lane_group = lax.broadcasted_iota(jnp.int32, (1, lane_tile), 1) // members
        lower = lower_ref[...]
        upper = upper_ref[...]
        mixed = jnp.zeros((tap_count, lane_tile), jnp.float32)
        for member in range(per_tile):
            part = jnp.dot(table_ref[member, :, :tap_count], lower, preferred_element_type=jnp.float32)
            part = part + jnp.dot(table_ref[member, :, tap_count:], upper, preferred_element_type=jnp.float32)
            mixed = jnp.where(lane_group == member, part, mixed)
        out_ref[...] = mixed

    grid = (channels // lane_tile, row_count // tap_count)
    return pl.pallas_call(
        body,
        grid=grid,
        in_specs=[
            pl.BlockSpec((per_tile, tap_count, window_rows), lambda j, n: (j, 0, 0)),
            pl.BlockSpec((tap_count, lane_tile), lambda j, n: (n, j)),
            pl.BlockSpec((tap_count, lane_tile), lambda j, n: (n + 1, j)),
        ],
        out_specs=pl.BlockSpec((tap_count, lane_tile), lambda j, n: (n, j)),
        out_shape=jax.ShapeDtypeStruct((row_count, channels), jnp.float32),
    )(table, padded_rows, padded_rows)


def per_device(query_in, key_in, value_in, feature_taps, filter_taps, out_weight, cotangent, ring):
    row_count, channels = query_in.shape
    tap_count = filter_taps.shape[1]
    tap_span = feature_taps.shape[0]
    full_cotangent = lax.all_gather(cotangent, "tp", axis=0, tiled=True)
    inputs = (query_in, key_in, value_in)
    before = passed_along(
        jnp.stack([rows[row_count - tap_span + 1 :] for rows in inputs], axis=0), "seq", 1
    )
    query_feat, key_feat, value_feat = (
        featurize(jnp.concatenate([before[i], inputs[i]], axis=0), feature_taps[:, i], row_count)
        for i in range(3)
    )
    mix_rows = (key_feat * value_feat).astype(jnp.bfloat16)
    mix_before = passed_along(mix_rows[row_count - tap_count :], "seq", 1)
    padded_mix = jnp.concatenate([mix_before, mix_rows], axis=0)
    long_conv = band_mix(padded_mix, band_table(filter_taps))
    gated_rows = (query_feat * long_conv).astype(jnp.bfloat16)
    seq_count = lax.axis_size("seq")
    grad_scale = (row_count * seq_count) ** (-0.5)

    projected = []

    def project(state):
        gated_rows, out_weight = state
        projected.append(
            lax.psum_scatter(
                jnp.dot(gated_rows, out_weight, preferred_element_type=jnp.float32).astype(
                    jnp.bfloat16
                ),
                "tp",
                scatter_dimension=0,
                tiled=True,
            )
        )
        return out_weight

    def gate_back(out_weight):
        grad_gated = lax.dot_general(
            full_cotangent, out_weight, (((1,), (1,)), ((), ())), preferred_element_type=jnp.float32
        )
        grad_conv = (grad_gated * query_feat).astype(jnp.bfloat16)
        grad_query = grad_gated * long_conv
        conv_after = passed_along(grad_conv[:tap_count], "seq", -1)
        return (grad_conv, conv_after, grad_query)

    def filter_back(state):
        grad_conv, conv_after, grad_query = state
        grad_mix = band_mix(
            jnp.concatenate([grad_conv, conv_after], axis=0), band_table(filter_taps, reverse=True)
        )
        grad_features = (grad_query, grad_mix * value_feat, grad_mix * key_feat)
        features_after = passed_along(
            jnp.stack([rows[: tap_span - 1] for rows in grad_features], axis=0).astype(jnp.bfloat16),
            "seq",
            -1,
        )
        return (grad_features, features_after)

    def feature_back(state):
        grad_features, features_after = state
        grads = tuple(
            spread_back(
                jnp.concatenate([grad_features[i], features_after[i].astype(jnp.float32)], axis=0),
                feature_taps[:, i],
                row_count,
            ).astype(jnp.bfloat16)
            for i in range(3)
        )
        return grads

    stages = [project, gate_back, filter_back, feature_back]
    state, summed_grad = ring_reduce_scatter(
        gated_rows, full_cotangent, grad_scale, ring, stages, (gated_rows, out_weight)
    )
    return (projected[0],) + state + (summed_grad,)


def ring_reduce_scatter(gated_rows, full_cotangent, grad_scale, ring, stages, state):
    count = len(ring)
    width = full_cotangent.shape[1] // count
    half = width // 2
    place_of = [0] * count
    for place, member in enumerate(ring):
        place_of[member] = place
    seq_index = lax.axis_index("seq")
    place = sum(jnp.where(seq_index == member, place_of[member], 0) for member in range(count))
    forward = [(ring[i], ring[(i + 1) % count]) for i in range(count)]
    backward = [(ring[(i + 1) % count], ring[i]) for i in range(count)]
    local_grad = (
        lax.dot_general(
            gated_rows, full_cotangent, (((0,), (0,)), ((), ())), preferred_element_type=jnp.float32
        )
        * grad_scale
    )

    def contribution(step, direction):
        position = (place - direction * (1 + step)) % count
        owner = sum(jnp.where(position == i, ring[i], 0) for i in range(count))
        first = owner * width + (0 if direction == 1 else half)
        return lax.dynamic_slice_in_dim(local_grad, first, half, 1)

    ahead = contribution(0, 1)
    behind = contribution(0, -1)
    stages = list(stages)
    for step in range(1, count):
        sent_ahead = ahead.astype(jnp.bfloat16)
        sent_behind = behind.astype(jnp.bfloat16)
        if stages:
            sent_ahead, sent_behind, state = lax.optimization_barrier(
                (sent_ahead, sent_behind, state)
            )
        ahead = lax.ppermute(sent_ahead, "seq", forward)
        behind = lax.ppermute(sent_behind, "seq", backward)
        if stages:
            state = stages.pop(0)(state)
            ahead, behind, state = lax.optimization_barrier((ahead, behind, state))
        ahead = ahead.astype(jnp.float32) + contribution(step, 1)
        behind = behind.astype(jnp.float32) + contribution(step, -1)
    while stages:
        state = stages.pop(0)(state)
    return state, jnp.concatenate([ahead, behind], axis=1).astype(jnp.bfloat16)


def ring_order(mesh):
    axis = mesh.axis_names.index("seq")
    members = jnp.moveaxis(jnp.arange(mesh.devices.size).reshape(mesh.devices.shape), axis, 0)
    devices = mesh.devices.reshape(-1)
    column = [devices[int(i)] for i in members[:, 0].reshape(-1)]
    count = len(column)
    try:
        coords = [tuple(d.coords) + (d.core_on_chip,) for d in column]
    except AttributeError:
        return list(range(count))
    varying = [k for k in range(len(coords[0])) if len({c[k] for c in coords}) > 1]
    if len(varying) != 2:
        return list(range(count))
    sizes = [len({c[k] for c in coords}) for k in varying]
    if 2 not in sizes or sizes[0] * sizes[1] != count:
        return list(range(count))
    short, long = (varying[0], varying[1]) if sizes[0] == 2 else (varying[1], varying[0])
    low_short = min(c[short] for c in coords)
    lanes = [[], []]
    for index, c in enumerate(coords):
        lanes[0 if c[short] == low_short else 1].append((c[long], index))
    return [i for _, i in sorted(lanes[0])] + [i for _, i in sorted(lanes[1], reverse=True)]


def solution(mesh):
    placed = (
        P("seq", "tp"),
        P("seq", "tp"),
        P("seq", "tp"),
        P(None, None, "tp"),
        P("tp", None),
        P("tp", None),
        P(("seq", "tp"), None),
    )
    ring = ring_order(mesh)
    return jax.shard_map(
        functools.partial(per_device, ring=ring),
        mesh=mesh,
        in_specs=placed,
        out_specs=(
            P(("seq", "tp"), None),
            P("seq", "tp"),
            P("seq", "tp"),
            P("seq", "tp"),
            P("tp", "seq"),
        ),
        check_vma=False,
    )
```

```python
import functools

import jax
import jax.numpy as jnp
from jax import lax
from jax.experimental import pallas as pl
from jax.sharding import PartitionSpec as P


def passed_along(value, axis, steps):
    count = lax.axis_size(axis)
    leading, last = (max(0, -steps), min(count, count - steps))
    return lax.ppermute(value, axis, [(source, source + steps) for source in range(leading, last)])


def featurize(extended, feature_taps, out_rows):
    tap_span = feature_taps.shape[0]
    summed = jnp.zeros((out_rows,) + extended.shape[1:], jnp.float32)
    for offset in range(tap_span):
        first_row = tap_span - 1 - offset
        summed = summed + feature_taps[offset] * extended[first_row : first_row + out_rows].astype(
            jnp.float32
        )
    return summed


def spread_back(extended, feature_taps, out_rows):
    tap_span = feature_taps.shape[0]
    summed = jnp.zeros((out_rows,) + extended.shape[1:], jnp.float32)
    for offset in range(tap_span):
        summed = summed + feature_taps[offset] * extended[offset : offset + out_rows]
    return summed


def band_table(filter_taps, reverse=False):
    tap_count = filter_taps.shape[1]
    window_rows = 2 * tap_count
    lag_index = jnp.arange(tap_count)[:, None, None]
    out_index = jnp.arange(tap_count)[None, :, None]
    row_index = jnp.arange(window_rows)[None, None, :]
    if reverse:
        select = (row_index - out_index == lag_index).astype(jnp.bfloat16)
    else:
        select = (out_index + tap_count - row_index == lag_index).astype(jnp.bfloat16)
    select = select.reshape(tap_count, tap_count * window_rows)
    table = jnp.dot(filter_taps, select, preferred_element_type=jnp.float32)
    return table.astype(jnp.bfloat16).reshape(filter_taps.shape[0], tap_count, window_rows)


def band_mix(padded_rows, table, lane_tile=128):
    group_count, tap_count, window_rows = table.shape
    row_count = padded_rows.shape[0] - tap_count
    block_count = row_count // tap_count
    channels = padded_rows.shape[1]
    members = channels // group_count
    per_tile = lane_tile // members

    def body(table_ref, rows_ref, out_ref):
        lane_group = lax.broadcasted_iota(jnp.int32, (1, lane_tile), 1) // members
        rows = rows_ref[...]
        window = jnp.concatenate(
            [rows[n * tap_count : n * tap_count + window_rows] for n in range(block_count)], axis=1
        )
        mixed = [jnp.zeros((tap_count, lane_tile), jnp.float32) for _ in range(block_count)]
        for member in range(per_tile):
            part = jnp.dot(table_ref[member], window, preferred_element_type=jnp.float32)
            for n in range(block_count):
                mixed[n] = jnp.where(
                    lane_group == member, part[:, n * lane_tile : (n + 1) * lane_tile], mixed[n]
                )
        for n in range(block_count):
            out_ref[n * tap_count : (n + 1) * tap_count, :] = mixed[n]

    return pl.pallas_call(
        body,
        grid=(channels // lane_tile,),
        in_specs=[
            pl.BlockSpec((per_tile, tap_count, window_rows), lambda j: (j, 0, 0)),
            pl.BlockSpec((row_count + tap_count, lane_tile), lambda j: (0, j)),
        ],
        out_specs=pl.BlockSpec((row_count, lane_tile), lambda j: (0, j)),
        out_shape=jax.ShapeDtypeStruct((row_count, channels), jnp.float32),
    )(table, padded_rows)


def per_device(query_in, key_in, value_in, feature_taps, filter_taps, out_weight, cotangent, ring):
    row_count, channels = query_in.shape
    tap_count = filter_taps.shape[1]
    tap_span = feature_taps.shape[0]
    full_cotangent = lax.all_gather(cotangent, "tp", axis=0, tiled=True)
    inputs = (query_in, key_in, value_in)
    before = passed_along(
        jnp.stack([rows[row_count - tap_span + 1 :] for rows in inputs], axis=0), "seq", 1
    )
    query_feat, key_feat, value_feat = (
        featurize(jnp.concatenate([before[i], inputs[i]], axis=0), feature_taps[:, i], row_count)
        for i in range(3)
    )
    mix_rows = (key_feat * value_feat).astype(jnp.bfloat16)
    mix_before = passed_along(mix_rows[row_count - tap_count :], "seq", 1)
    padded_mix = jnp.concatenate([mix_before, mix_rows], axis=0)
    long_conv = band_mix(padded_mix, band_table(filter_taps))
    gated_rows = (query_feat * long_conv).astype(jnp.bfloat16)
    seq_count = lax.axis_size("seq")
    grad_scale = (row_count * seq_count) ** (-0.5)

    projected = []

    def project(state):
        gated_rows, out_weight = state
        projected.append(
            lax.psum_scatter(
                jnp.dot(gated_rows, out_weight, preferred_element_type=jnp.float32).astype(
                    jnp.bfloat16
                ),
                "tp",
                scatter_dimension=0,
                tiled=True,
            )
        )
        return out_weight

    def gate_back(out_weight):
        grad_gated = lax.dot_general(
            full_cotangent, out_weight, (((1,), (1,)), ((), ())), preferred_element_type=jnp.float32
        )
        grad_conv = (grad_gated * query_feat).astype(jnp.bfloat16)
        grad_query = grad_gated * long_conv
        conv_after = passed_along(grad_conv[:tap_count], "seq", -1)
        return (grad_conv, conv_after, grad_query)

    def filter_back(state):
        grad_conv, conv_after, grad_query = state
        grad_mix = band_mix(
            jnp.concatenate([grad_conv, conv_after], axis=0), band_table(filter_taps, reverse=True)
        )
        grad_features = (grad_query, grad_mix * value_feat, grad_mix * key_feat)
        features_after = passed_along(
            jnp.stack([rows[: tap_span - 1] for rows in grad_features], axis=0).astype(jnp.bfloat16),
            "seq",
            -1,
        )
        return (grad_features, features_after)

    def feature_back(state):
        grad_features, features_after = state
        grads = tuple(
            spread_back(
                jnp.concatenate([grad_features[i], features_after[i].astype(jnp.float32)], axis=0),
                feature_taps[:, i],
                row_count,
            ).astype(jnp.bfloat16)
            for i in range(3)
        )
        return grads

    stages = [project, gate_back, filter_back, feature_back]
    state, summed_grad = ring_reduce_scatter(
        gated_rows, full_cotangent, grad_scale, ring, stages, (gated_rows, out_weight)
    )
    return (projected[0],) + state + (summed_grad,)


def ring_reduce_scatter(gated_rows, full_cotangent, grad_scale, ring, stages, state):
    count = len(ring)
    width = full_cotangent.shape[1] // count
    half = width // 2
    place_of = [0] * count
    for place, member in enumerate(ring):
        place_of[member] = place
    seq_index = lax.axis_index("seq")
    place = sum(jnp.where(seq_index == member, place_of[member], 0) for member in range(count))
    forward = [(ring[i], ring[(i + 1) % count]) for i in range(count)]
    backward = [(ring[(i + 1) % count], ring[i]) for i in range(count)]
    local_grad = (
        lax.dot_general(
            gated_rows, full_cotangent, (((0,), (0,)), ((), ())), preferred_element_type=jnp.float32
        )
        * grad_scale
    )

    def contribution(step, direction):
        position = (place - direction * (1 + step)) % count
        owner = sum(jnp.where(position == i, ring[i], 0) for i in range(count))
        first = owner * width + (0 if direction == 1 else half)
        return lax.dynamic_slice_in_dim(local_grad, first, half, 1)

    ahead = contribution(0, 1)
    behind = contribution(0, -1)
    stages = list(stages)
    for step in range(1, count):
        sent_ahead = ahead.astype(jnp.bfloat16)
        sent_behind = behind.astype(jnp.bfloat16)
        if stages:
            sent_ahead, sent_behind, state = lax.optimization_barrier(
                (sent_ahead, sent_behind, state)
            )
        ahead = lax.ppermute(sent_ahead, "seq", forward)
        behind = lax.ppermute(sent_behind, "seq", backward)
        if stages:
            state = stages.pop(0)(state)
            ahead, behind, state = lax.optimization_barrier((ahead, behind, state))
        ahead = ahead.astype(jnp.float32) + contribution(step, 1)
        behind = behind.astype(jnp.float32) + contribution(step, -1)
    while stages:
        state = stages.pop(0)(state)
    return state, jnp.concatenate([ahead, behind], axis=1).astype(jnp.bfloat16)


def ring_order(mesh):
    axis = mesh.axis_names.index("seq")
    members = jnp.moveaxis(jnp.arange(mesh.devices.size).reshape(mesh.devices.shape), axis, 0)
    devices = mesh.devices.reshape(-1)
    column = [devices[int(i)] for i in members[:, 0].reshape(-1)]
    count = len(column)
    try:
        coords = [tuple(d.coords) + (d.core_on_chip,) for d in column]
    except AttributeError:
        return list(range(count))
    varying = [k for k in range(len(coords[0])) if len({c[k] for c in coords}) > 1]
    if len(varying) != 2:
        return list(range(count))
    sizes = [len({c[k] for c in coords}) for k in varying]
    if 2 not in sizes or sizes[0] * sizes[1] != count:
        return list(range(count))
    short, long = (varying[0], varying[1]) if sizes[0] == 2 else (varying[1], varying[0])
    low_short = min(c[short] for c in coords)
    lanes = [[], []]
    for index, c in enumerate(coords):
        lanes[0 if c[short] == low_short else 1].append((c[long], index))
    return [i for _, i in sorted(lanes[0])] + [i for _, i in sorted(lanes[1], reverse=True)]


def solution(mesh):
    placed = (
        P("seq", "tp"),
        P("seq", "tp"),
        P("seq", "tp"),
        P(None, None, "tp"),
        P("tp", None),
        P("tp", None),
        P(("seq", "tp"), None),
    )
    ring = ring_order(mesh)
    return jax.shard_map(
        functools.partial(per_device, ring=ring),
        mesh=mesh,
        in_specs=placed,
        out_specs=(
            P(("seq", "tp"), None),
            P("seq", "tp"),
            P("seq", "tp"),
            P("seq", "tp"),
            P("tp", "seq"),
        ),
        check_vma=False,
    )
```

```python
import functools

import jax
import jax.numpy as jnp
from jax import lax
from jax.experimental import pallas as pl
from jax.sharding import PartitionSpec as P


def passed_along(value, axis, steps):
    count = lax.axis_size(axis)
    leading, last = (max(0, -steps), min(count, count - steps))
    return lax.ppermute(value, axis, [(source, source + steps) for source in range(leading, last)])


def featurize(extended, feature_taps, out_rows):
    tap_span = feature_taps.shape[0]
    summed = jnp.zeros((out_rows,) + extended.shape[1:], jnp.float32)
    for offset in range(tap_span):
        first_row = tap_span - 1 - offset
        summed = summed + feature_taps[offset] * extended[first_row : first_row + out_rows].astype(
            jnp.float32
        )
    return summed


def spread_back(extended, feature_taps, out_rows):
    tap_span = feature_taps.shape[0]
    summed = jnp.zeros((out_rows,) + extended.shape[1:], jnp.float32)
    for offset in range(tap_span):
        summed = summed + feature_taps[offset] * extended[offset : offset + out_rows]
    return summed


def band_table(filter_taps, reverse=False):
    tap_count = filter_taps.shape[1]
    window_rows = 2 * tap_count
    lag_index = jnp.arange(tap_count)[:, None, None]
    out_index = jnp.arange(tap_count)[None, :, None]
    row_index = jnp.arange(window_rows)[None, None, :]
    if reverse:
        select = (row_index - out_index == lag_index).astype(jnp.bfloat16)
    else:
        select = (out_index + tap_count - row_index == lag_index).astype(jnp.bfloat16)
    select = select.reshape(tap_count, tap_count * window_rows)
    table = jnp.dot(filter_taps, select, preferred_element_type=jnp.float32)
    return table.astype(jnp.bfloat16).reshape(filter_taps.shape[0], tap_count, window_rows)


def band_mix(padded_rows, table, lane_tile=128):
    group_count, tap_count, window_rows = table.shape
    row_count = padded_rows.shape[0] - tap_count
    block_count = row_count // tap_count
    channels = padded_rows.shape[1]
    members = channels // group_count
    per_tile = lane_tile // members

    def body(table_ref, rows_ref, out_ref):
        lane_group = lax.broadcasted_iota(jnp.int32, (1, lane_tile), 1) // members
        rows = rows_ref[...]
        window = jnp.concatenate(
            [rows[n * tap_count : n * tap_count + window_rows] for n in range(block_count)], axis=1
        )
        mixed = [jnp.zeros((tap_count, lane_tile), jnp.float32) for _ in range(block_count)]
        for member in range(per_tile):
            part = jnp.dot(table_ref[member], window, preferred_element_type=jnp.float32)
            for n in range(block_count):
                mixed[n] = jnp.where(
                    lane_group == member, part[:, n * lane_tile : (n + 1) * lane_tile], mixed[n]
                )
        for n in range(block_count):
            out_ref[n * tap_count : (n + 1) * tap_count, :] = mixed[n]

    return pl.pallas_call(
        body,
        grid=(channels // lane_tile,),
        in_specs=[
            pl.BlockSpec((per_tile, tap_count, window_rows), lambda j: (j, 0, 0)),
            pl.BlockSpec((row_count + tap_count, lane_tile), lambda j: (0, j)),
        ],
        out_specs=pl.BlockSpec((row_count, lane_tile), lambda j: (0, j)),
        out_shape=jax.ShapeDtypeStruct((row_count, channels), jnp.float32),
    )(table, padded_rows)


def per_device(query_in, key_in, value_in, feature_taps, filter_taps, out_weight, cotangent, ring):
    row_count, channels = query_in.shape
    tap_count = filter_taps.shape[1]
    tap_span = feature_taps.shape[0]
    full_cotangent = lax.all_gather(cotangent, "tp", axis=0, tiled=True)
    inputs = (query_in, key_in, value_in)
    before = passed_along(
        jnp.stack([rows[row_count - tap_span + 1 :] for rows in inputs], axis=0), "seq", 1
    )
    query_feat, key_feat, value_feat = (
        featurize(jnp.concatenate([before[i], inputs[i]], axis=0), feature_taps[:, i], row_count)
        for i in range(3)
    )
    mix_rows = (key_feat * value_feat).astype(jnp.bfloat16)
    mix_before = passed_along(mix_rows[row_count - tap_count :], "seq", 1)
    padded_mix = jnp.concatenate([mix_before, mix_rows], axis=0)
    long_conv = band_mix(padded_mix, band_table(filter_taps))
    gated_rows = (query_feat * long_conv).astype(jnp.bfloat16)
    seq_count = lax.axis_size("seq")
    grad_scale = (row_count * seq_count) ** (-0.5)

    projected = []

    def project(state):
        gated_rows, out_weight = state
        projected.append(
            lax.psum_scatter(
                jnp.dot(gated_rows, out_weight, preferred_element_type=jnp.float32).astype(
                    jnp.bfloat16
                ),
                "tp",
                scatter_dimension=0,
                tiled=True,
            )
        )
        return out_weight

    def gate_back(out_weight):
        grad_gated = lax.dot_general(
            full_cotangent, out_weight, (((1,), (1,)), ((), ())), preferred_element_type=jnp.float32
        )
        grad_conv = (grad_gated * query_feat).astype(jnp.bfloat16)
        grad_query = grad_gated * long_conv
        conv_after = passed_along(grad_conv[:tap_count], "seq", -1)
        return (grad_conv, conv_after, grad_query)

    def filter_back(state):
        grad_conv, conv_after, grad_query = state
        grad_mix = band_mix(
            jnp.concatenate([grad_conv, conv_after], axis=0), band_table(filter_taps, reverse=True)
        )
        grad_features = (grad_query, grad_mix * value_feat, grad_mix * key_feat)
        features_after = passed_along(
            jnp.stack([rows[: tap_span - 1] for rows in grad_features], axis=0).astype(jnp.bfloat16),
            "seq",
            -1,
        )
        return (grad_features, features_after)

    def feature_back(state):
        grad_features, features_after = state
        grads = tuple(
            spread_back(
                jnp.concatenate([grad_features[i], features_after[i].astype(jnp.float32)], axis=0),
                feature_taps[:, i],
                row_count,
            ).astype(jnp.bfloat16)
            for i in range(3)
        )
        return grads

    stages = [project, gate_back, filter_back, feature_back]
    state, summed_grad = ring_reduce_scatter(
        gated_rows, full_cotangent, grad_scale, ring, stages, (gated_rows, out_weight)
    )
    return (projected[0],) + state + (summed_grad,)


def ring_reduce_scatter(gated_rows, full_cotangent, grad_scale, ring, stages, state):
    count = len(ring)
    width = full_cotangent.shape[1] // count
    half = width // 2
    place_of = [0] * count
    for place, member in enumerate(ring):
        place_of[member] = place
    seq_index = lax.axis_index("seq")
    place = sum(jnp.where(seq_index == member, place_of[member], 0) for member in range(count))
    forward = [(ring[i], ring[(i + 1) % count]) for i in range(count)]
    backward = [(ring[(i + 1) % count], ring[i]) for i in range(count)]
    def contribution(step, direction, gated_rows):
        position = (place - direction * (1 + step)) % count
        owner = sum(jnp.where(position == i, ring[i], 0) for i in range(count))
        first = owner * width + (0 if direction == 1 else half)
        columns = lax.dynamic_slice_in_dim(full_cotangent, first, half, 1)
        return (
            lax.dot_general(
                gated_rows, columns, (((0,), (0,)), ((), ())), preferred_element_type=jnp.float32
            )
            * grad_scale
        )

    ahead = contribution(0, 1, gated_rows)
    behind = contribution(0, -1, gated_rows)
    stages = list(stages)
    for step in range(1, count):
        sent_ahead, sent_behind, state, rows = lax.optimization_barrier(
            (ahead.astype(jnp.bfloat16), behind.astype(jnp.bfloat16), state, gated_rows)
        )
        ahead = lax.ppermute(sent_ahead, "seq", forward)
        behind = lax.ppermute(sent_behind, "seq", backward)
        if stages:
            state = stages.pop(0)(state)
        more_ahead = contribution(step, 1, rows)
        more_behind = contribution(step, -1, rows)
        ahead, behind, state, more_ahead, more_behind = lax.optimization_barrier(
            (ahead, behind, state, more_ahead, more_behind)
        )
        ahead = ahead.astype(jnp.float32) + more_ahead
        behind = behind.astype(jnp.float32) + more_behind
    while stages:
        state = stages.pop(0)(state)
    return state, jnp.concatenate([ahead, behind], axis=1).astype(jnp.bfloat16)


def ring_order(mesh):
    axis = mesh.axis_names.index("seq")
    members = jnp.moveaxis(jnp.arange(mesh.devices.size).reshape(mesh.devices.shape), axis, 0)
    devices = mesh.devices.reshape(-1)
    column = [devices[int(i)] for i in members[:, 0].reshape(-1)]
    count = len(column)
    try:
        coords = [tuple(d.coords) + (d.core_on_chip,) for d in column]
    except AttributeError:
        return list(range(count))
    varying = [k for k in range(len(coords[0])) if len({c[k] for c in coords}) > 1]
    if len(varying) != 2:
        return list(range(count))
    sizes = [len({c[k] for c in coords}) for k in varying]
    if 2 not in sizes or sizes[0] * sizes[1] != count:
        return list(range(count))
    short, long = (varying[0], varying[1]) if sizes[0] == 2 else (varying[1], varying[0])
    low_short = min(c[short] for c in coords)
    lanes = [[], []]
    for index, c in enumerate(coords):
        lanes[0 if c[short] == low_short else 1].append((c[long], index))
    return [i for _, i in sorted(lanes[0])] + [i for _, i in sorted(lanes[1], reverse=True)]


def solution(mesh):
    placed = (
        P("seq", "tp"),
        P("seq", "tp"),
        P("seq", "tp"),
        P(None, None, "tp"),
        P("tp", None),
        P("tp", None),
        P(("seq", "tp"), None),
    )
    ring = ring_order(mesh)
    return jax.shard_map(
        functools.partial(per_device, ring=ring),
        mesh=mesh,
        in_specs=placed,
        out_specs=(
            P(("seq", "tp"), None),
            P("seq", "tp"),
            P("seq", "tp"),
            P("seq", "tp"),
            P("tp", "seq"),
        ),
        check_vma=False,
    )
```

```python
import functools

import jax
import jax.numpy as jnp
from jax import lax
from jax.experimental import pallas as pl
from jax.sharding import PartitionSpec as P


def passed_along(value, axis, steps):
    count = lax.axis_size(axis)
    leading, last = (max(0, -steps), min(count, count - steps))
    return lax.ppermute(value, axis, [(source, source + steps) for source in range(leading, last)])


def featurize(extended, feature_taps, out_rows):
    tap_span = feature_taps.shape[0]
    summed = jnp.zeros((out_rows,) + extended.shape[1:], jnp.float32)
    for offset in range(tap_span):
        first_row = tap_span - 1 - offset
        summed = summed + feature_taps[offset] * extended[first_row : first_row + out_rows].astype(
            jnp.float32
        )
    return summed


def spread_back(extended, feature_taps, out_rows):
    tap_span = feature_taps.shape[0]
    summed = jnp.zeros((out_rows,) + extended.shape[1:], jnp.float32)
    for offset in range(tap_span):
        summed = summed + feature_taps[offset] * extended[offset : offset + out_rows]
    return summed


def band_table(filter_taps, reverse=False):
    tap_count = filter_taps.shape[1]
    window_rows = 2 * tap_count
    lag_index = jnp.arange(tap_count)[:, None, None]
    out_index = jnp.arange(tap_count)[None, :, None]
    row_index = jnp.arange(window_rows)[None, None, :]
    if reverse:
        select = (row_index - out_index == lag_index).astype(jnp.bfloat16)
    else:
        select = (out_index + tap_count - row_index == lag_index).astype(jnp.bfloat16)
    select = select.reshape(tap_count, tap_count * window_rows)
    table = jnp.dot(filter_taps, select, preferred_element_type=jnp.float32)
    return table.astype(jnp.bfloat16).reshape(filter_taps.shape[0], tap_count, window_rows)


def band_mix(padded_rows, table, lane_tile=128):
    group_count, tap_count, window_rows = table.shape
    row_count = padded_rows.shape[0] - tap_count
    block_count = row_count // tap_count
    channels = padded_rows.shape[1]
    members = channels // group_count
    per_tile = lane_tile // members

    def body(table_ref, rows_ref, out_ref):
        lane_group = lax.broadcasted_iota(jnp.int32, (1, lane_tile), 1) // members
        rows = rows_ref[...]
        window = jnp.concatenate(
            [rows[n * tap_count : n * tap_count + window_rows] for n in range(block_count)], axis=1
        )
        mixed = [jnp.zeros((tap_count, lane_tile), jnp.float32) for _ in range(block_count)]
        for member in range(per_tile):
            part = jnp.dot(table_ref[member], window, preferred_element_type=jnp.float32)
            for n in range(block_count):
                mixed[n] = jnp.where(
                    lane_group == member, part[:, n * lane_tile : (n + 1) * lane_tile], mixed[n]
                )
        for n in range(block_count):
            out_ref[n * tap_count : (n + 1) * tap_count, :] = mixed[n]

    return pl.pallas_call(
        body,
        grid=(channels // lane_tile,),
        in_specs=[
            pl.BlockSpec((per_tile, tap_count, window_rows), lambda j: (j, 0, 0)),
            pl.BlockSpec((row_count + tap_count, lane_tile), lambda j: (0, j)),
        ],
        out_specs=pl.BlockSpec((row_count, lane_tile), lambda j: (0, j)),
        out_shape=jax.ShapeDtypeStruct((row_count, channels), jnp.float32),
    )(table, padded_rows)


def per_device(query_in, key_in, value_in, feature_taps, filter_taps, out_weight, cotangent, ring):
    row_count, channels = query_in.shape
    tap_count = filter_taps.shape[1]
    tap_span = feature_taps.shape[0]
    full_cotangent = lax.all_gather(cotangent, "tp", axis=0, tiled=True)
    inputs = (query_in, key_in, value_in)
    before = passed_along(
        jnp.stack([rows[row_count - tap_span + 1 :] for rows in inputs], axis=0), "seq", 1
    )
    query_feat, key_feat, value_feat = (
        featurize(jnp.concatenate([before[i], inputs[i]], axis=0), feature_taps[:, i], row_count)
        for i in range(3)
    )
    mix_rows = (key_feat * value_feat).astype(jnp.bfloat16)
    mix_before = passed_along(mix_rows[row_count - tap_count :], "seq", 1)
    padded_mix = jnp.concatenate([mix_before, mix_rows], axis=0)
    long_conv = band_mix(padded_mix, band_table(filter_taps))
    gated_rows = (query_feat * long_conv).astype(jnp.bfloat16)
    seq_count = lax.axis_size("seq")
    grad_scale = (row_count * seq_count) ** (-0.5)

    projected = []

    def project(state):
        gated_rows, out_weight = state
        projected.append(
            lax.psum_scatter(
                jnp.dot(gated_rows, out_weight, preferred_element_type=jnp.float32).astype(
                    jnp.bfloat16
                ),
                "tp",
                scatter_dimension=0,
                tiled=True,
            )
        )
        return out_weight

    def gate_back(out_weight):
        grad_gated = lax.dot_general(
            full_cotangent, out_weight, (((1,), (1,)), ((), ())), preferred_element_type=jnp.float32
        )
        grad_conv = (grad_gated * query_feat).astype(jnp.bfloat16)
        grad_query = grad_gated * long_conv
        conv_after = passed_along(grad_conv[:tap_count], "seq", -1)
        return (grad_conv, conv_after, grad_query)

    def table_back(state):
        return state + (band_table(filter_taps, reverse=True),)

    def filter_back(state):
        grad_conv, conv_after, grad_query, table = state
        grad_mix = band_mix(jnp.concatenate([grad_conv, conv_after], axis=0), table)
        grad_features = (grad_query, grad_mix * value_feat, grad_mix * key_feat)
        features_after = passed_along(
            jnp.stack([rows[: tap_span - 1] for rows in grad_features], axis=0).astype(jnp.bfloat16),
            "seq",
            -1,
        )
        return (grad_features, features_after)

    def feature_back(first, last):
        def stage(state):
            grad_features, features_after, done = state
            grads = tuple(
                spread_back(
                    jnp.concatenate(
                        [grad_features[i], features_after[i].astype(jnp.float32)], axis=0
                    ),
                    feature_taps[:, i],
                    row_count,
                ).astype(jnp.bfloat16)
                for i in range(first, last)
            )
            return (grad_features, features_after, done + grads)

        return stage

    def finish(state):
        return state[2]

    def unpack(state):
        grad_features, features_after = state
        return (grad_features, features_after, ())

    stages = [
        project,
        gate_back,
        table_back,
        filter_back,
        lambda state: feature_back(0, 1)(unpack(state)),
        feature_back(1, 3),
        finish,
    ]
    state, summed_grad = ring_reduce_scatter(
        gated_rows, full_cotangent, grad_scale, ring, stages, (gated_rows, out_weight)
    )
    return (projected[0],) + state + (summed_grad,)


def ring_reduce_scatter(gated_rows, full_cotangent, grad_scale, ring, stages, state):
    count = len(ring)
    width = full_cotangent.shape[1] // count
    half = width // 2
    place_of = [0] * count
    for place, member in enumerate(ring):
        place_of[member] = place
    seq_index = lax.axis_index("seq")
    place = sum(jnp.where(seq_index == member, place_of[member], 0) for member in range(count))
    forward = [(ring[i], ring[(i + 1) % count]) for i in range(count)]
    backward = [(ring[(i + 1) % count], ring[i]) for i in range(count)]
    local_grad = (
        lax.dot_general(
            gated_rows, full_cotangent, (((0,), (0,)), ((), ())), preferred_element_type=jnp.float32
        )
        * grad_scale
    ).astype(jnp.bfloat16)

    def contribution(step, direction):
        position = (place - direction * (1 + step)) % count
        owner = sum(jnp.where(position == i, ring[i], 0) for i in range(count))
        first = owner * width + (0 if direction == 1 else half)
        return lax.dynamic_slice_in_dim(local_grad, first, half, 1)

    ahead = contribution(0, 1)
    behind = contribution(0, -1)
    stages = list(stages)
    for step in range(1, count):
        sent_ahead = ahead.astype(jnp.bfloat16)
        sent_behind = behind.astype(jnp.bfloat16)
        if stages:
            sent_ahead, sent_behind, state = lax.optimization_barrier(
                (sent_ahead, sent_behind, state)
            )
        ahead = lax.ppermute(sent_ahead, "seq", forward)
        behind = lax.ppermute(sent_behind, "seq", backward)
        if stages:
            state = stages.pop(0)(state)
            ahead, behind, state = lax.optimization_barrier((ahead, behind, state))
        ahead = ahead.astype(jnp.float32) + contribution(step, 1).astype(jnp.float32)
        behind = behind.astype(jnp.float32) + contribution(step, -1).astype(jnp.float32)
    while stages:
        state = stages.pop(0)(state)
    return state, jnp.concatenate([ahead, behind], axis=1).astype(jnp.bfloat16)


def ring_order(mesh):
    axis = mesh.axis_names.index("seq")
    members = jnp.moveaxis(jnp.arange(mesh.devices.size).reshape(mesh.devices.shape), axis, 0)
    devices = mesh.devices.reshape(-1)
    column = [devices[int(i)] for i in members[:, 0].reshape(-1)]
    count = len(column)
    try:
        coords = [tuple(d.coords) + (d.core_on_chip,) for d in column]
    except AttributeError:
        return list(range(count))
    varying = [k for k in range(len(coords[0])) if len({c[k] for c in coords}) > 1]
    if len(varying) != 2:
        return list(range(count))
    sizes = [len({c[k] for c in coords}) for k in varying]
    if 2 not in sizes or sizes[0] * sizes[1] != count:
        return list(range(count))
    short, long = (varying[0], varying[1]) if sizes[0] == 2 else (varying[1], varying[0])
    low_short = min(c[short] for c in coords)
    lanes = [[], []]
    for index, c in enumerate(coords):
        lanes[0 if c[short] == low_short else 1].append((c[long], index))
    return [i for _, i in sorted(lanes[0])] + [i for _, i in sorted(lanes[1], reverse=True)]


def solution(mesh):
    placed = (
        P("seq", "tp"),
        P("seq", "tp"),
        P("seq", "tp"),
        P(None, None, "tp"),
        P("tp", None),
        P("tp", None),
        P(("seq", "tp"), None),
    )
    ring = ring_order(mesh)
    return jax.shard_map(
        functools.partial(per_device, ring=ring),
        mesh=mesh,
        in_specs=placed,
        out_specs=(
            P(("seq", "tp"), None),
            P("seq", "tp"),
            P("seq", "tp"),
            P("seq", "tp"),
            P("tp", "seq"),
        ),
        check_vma=False,
    )
```

```python
import functools

import jax
import jax.numpy as jnp
from jax import lax
from jax.experimental import pallas as pl
from jax.sharding import PartitionSpec as P


def passed_along(value, axis, steps):
    count = lax.axis_size(axis)
    leading, last = (max(0, -steps), min(count, count - steps))
    return lax.ppermute(value, axis, [(source, source + steps) for source in range(leading, last)])


def featurize(extended, feature_taps, out_rows):
    tap_span = feature_taps.shape[0]
    summed = jnp.zeros((out_rows,) + extended.shape[1:], jnp.float32)
    for offset in range(tap_span):
        first_row = tap_span - 1 - offset
        summed = summed + feature_taps[offset] * extended[first_row : first_row + out_rows].astype(
            jnp.float32
        )
    return summed


def spread_back(extended, feature_taps, out_rows):
    tap_span = feature_taps.shape[0]
    summed = jnp.zeros((out_rows,) + extended.shape[1:], jnp.float32)
    for offset in range(tap_span):
        summed = summed + feature_taps[offset] * extended[offset : offset + out_rows]
    return summed


def band_table(filter_taps, reverse=False):
    tap_count = filter_taps.shape[1]
    window_rows = 2 * tap_count
    lag_index = jnp.arange(tap_count)[:, None, None]
    out_index = jnp.arange(tap_count)[None, :, None]
    row_index = jnp.arange(window_rows)[None, None, :]
    if reverse:
        select = (row_index - out_index == lag_index).astype(jnp.bfloat16)
    else:
        select = (out_index + tap_count - row_index == lag_index).astype(jnp.bfloat16)
    select = select.reshape(tap_count, tap_count * window_rows)
    table = jnp.dot(filter_taps, select, preferred_element_type=jnp.float32)
    return table.astype(jnp.bfloat16).reshape(filter_taps.shape[0], tap_count, window_rows)


def band_mix(padded_rows, table, lane_tile=128):
    group_count, tap_count, window_rows = table.shape
    row_count = padded_rows.shape[0] - tap_count
    block_count = row_count // tap_count
    channels = padded_rows.shape[1]
    members = channels // group_count
    per_tile = lane_tile // members

    def body(table_ref, rows_ref, out_ref):
        lane_group = lax.broadcasted_iota(jnp.int32, (1, lane_tile), 1) // members
        rows = rows_ref[...]
        window = jnp.concatenate(
            [rows[n * tap_count : n * tap_count + window_rows] for n in range(block_count)], axis=1
        )
        mixed = [jnp.zeros((tap_count, lane_tile), jnp.float32) for _ in range(block_count)]
        for member in range(per_tile):
            part = jnp.dot(table_ref[member], window, preferred_element_type=jnp.float32)
            for n in range(block_count):
                mixed[n] = jnp.where(
                    lane_group == member, part[:, n * lane_tile : (n + 1) * lane_tile], mixed[n]
                )
        for n in range(block_count):
            out_ref[n * tap_count : (n + 1) * tap_count, :] = mixed[n]

    return pl.pallas_call(
        body,
        grid=(channels // lane_tile,),
        in_specs=[
            pl.BlockSpec((per_tile, tap_count, window_rows), lambda j: (j, 0, 0)),
            pl.BlockSpec((row_count + tap_count, lane_tile), lambda j: (0, j)),
        ],
        out_specs=pl.BlockSpec((row_count, lane_tile), lambda j: (0, j)),
        out_shape=jax.ShapeDtypeStruct((row_count, channels), jnp.float32),
    )(table, padded_rows)


def per_device(query_in, key_in, value_in, feature_taps, filter_taps, out_weight, cotangent, ring):
    row_count, channels = query_in.shape
    tap_count = filter_taps.shape[1]
    tap_span = feature_taps.shape[0]
    full_cotangent = lax.all_gather(cotangent, "tp", axis=0, tiled=True)
    reach = tap_count + tap_span - 1
    query_before = passed_along(query_in[row_count - tap_span + 1 :], "seq", 1)
    pair_before = passed_along(
        jnp.stack([key_in[row_count - reach :], value_in[row_count - reach :]], axis=0), "seq", 1
    )
    query_feat = featurize(
        jnp.concatenate([query_before, query_in], axis=0), feature_taps[:, 0], row_count
    )
    key_wide, value_wide = (
        featurize(
            jnp.concatenate([pair_before[i], rows], axis=0),
            feature_taps[:, i + 1],
            row_count + tap_count,
        )
        for i, rows in enumerate((key_in, value_in))
    )
    padded_mix = (key_wide * value_wide).astype(jnp.bfloat16)
    key_feat = key_wide[tap_count:]
    value_feat = value_wide[tap_count:]
    long_conv = band_mix(padded_mix, band_table(filter_taps))
    gated_rows = (query_feat * long_conv).astype(jnp.bfloat16)
    seq_count = lax.axis_size("seq")
    grad_scale = (row_count * seq_count) ** (-0.5)

    projected = []

    def project(state):
        gated_rows, out_weight = state
        projected.append(
            lax.psum_scatter(
                jnp.dot(gated_rows, out_weight, preferred_element_type=jnp.float32).astype(
                    jnp.bfloat16
                ),
                "tp",
                scatter_dimension=0,
                tiled=True,
            )
        )
        return out_weight

    def gate_back(out_weight):
        grad_gated = lax.dot_general(
            full_cotangent, out_weight, (((1,), (1,)), ((), ())), preferred_element_type=jnp.float32
        )
        grad_conv = (grad_gated * query_feat).astype(jnp.bfloat16)
        grad_query = grad_gated * long_conv
        conv_after = passed_along(grad_conv[:tap_count], "seq", -1)
        return (grad_conv, conv_after, grad_query, out_weight)

    def table_back(state):
        return state + (band_table(filter_taps, reverse=True),)

    def filter_back(state):
        grad_conv, conv_after, grad_query, out_weight, table = state
        grad_mix = band_mix(jnp.concatenate([grad_conv, conv_after], axis=0), table)
        grad_features = (grad_query, grad_mix * value_feat, grad_mix * key_feat)
        features_after = passed_along(
            jnp.stack([rows[: tap_span - 1] for rows in grad_features], axis=0).astype(jnp.bfloat16),
            "seq",
            -1,
        )
        return (grad_features, features_after, out_weight)

    def feature_back(first, last):
        def stage(state):
            grad_features, features_after, done = state
            grads = tuple(
                spread_back(
                    jnp.concatenate(
                        [grad_features[i], features_after[i].astype(jnp.float32)], axis=0
                    ),
                    feature_taps[:, i],
                    row_count,
                ).astype(jnp.bfloat16)
                for i in range(first, last)
            )
            return (grad_features, features_after, done + grads)

        return stage

    def finish(state):
        return state[2]

    def unpack(state):
        grad_features, features_after = state
        return (grad_features, features_after, ())

    def start_back(out_weight):
        return out_weight

    stages = [
        start_back,
        gate_back,
        table_back,
        filter_back,
        lambda state: (project((gated_rows, state[2])), state[:2])[1],
        lambda state: feature_back(0, 2)(unpack(state)),
        lambda state: finish(feature_back(2, 3)(state)),
    ]
    state, summed_grad = ring_reduce_scatter(
        gated_rows, full_cotangent, grad_scale, ring, stages, out_weight
    )
    return (projected[0],) + state + (summed_grad,)


def ring_reduce_scatter(gated_rows, full_cotangent, grad_scale, ring, stages, state):
    count = len(ring)
    width = full_cotangent.shape[1] // count
    half = width // 2
    place_of = [0] * count
    for place, member in enumerate(ring):
        place_of[member] = place
    seq_index = lax.axis_index("seq")
    place = sum(jnp.where(seq_index == member, place_of[member], 0) for member in range(count))
    forward = [(ring[i], ring[(i + 1) % count]) for i in range(count)]
    backward = [(ring[(i + 1) % count], ring[i]) for i in range(count)]
    def product(rows, columns):
        return (
            lax.dot_general(
                rows, columns, (((0,), (0,)), ((), ())), preferred_element_type=jnp.float32
            )
            * grad_scale
        ).astype(jnp.bfloat16)

    def column_of(step, direction):
        position = (place - direction * (1 + step)) % count
        owner = sum(jnp.where(position == i, ring[i], 0) for i in range(count))
        return owner * width + (0 if direction == 1 else half)

    def first_slice(direction):
        columns = lax.dynamic_slice_in_dim(full_cotangent, column_of(0, direction), half, 1)
        return product(gated_rows, columns).astype(jnp.float32)

    ahead = first_slice(1)
    behind = first_slice(-1)
    stages = list(stages)
    local_grad = None
    for step in range(1, count):
        sent_ahead = ahead.astype(jnp.bfloat16)
        sent_behind = behind.astype(jnp.bfloat16)
        sent_ahead, sent_behind, state, rows = lax.optimization_barrier(
            (sent_ahead, sent_behind, state, gated_rows)
        )
        ahead = lax.ppermute(sent_ahead, "seq", forward)
        behind = lax.ppermute(sent_behind, "seq", backward)
        if local_grad is None:
            local_grad = product(rows, full_cotangent)
        if stages:
            state = stages.pop(0)(state)
        ahead, behind, state, local_grad = lax.optimization_barrier(
            (ahead, behind, state, local_grad)
        )
        ahead = ahead.astype(jnp.float32) + lax.dynamic_slice_in_dim(
            local_grad, column_of(step, 1), half, 1
        ).astype(jnp.float32)
        behind = behind.astype(jnp.float32) + lax.dynamic_slice_in_dim(
            local_grad, column_of(step, -1), half, 1
        ).astype(jnp.float32)
    while stages:
        state = stages.pop(0)(state)
    return state, jnp.concatenate([ahead, behind], axis=1).astype(jnp.bfloat16)


def ring_order(mesh):
    axis = mesh.axis_names.index("seq")
    members = jnp.moveaxis(jnp.arange(mesh.devices.size).reshape(mesh.devices.shape), axis, 0)
    devices = mesh.devices.reshape(-1)
    column = [devices[int(i)] for i in members[:, 0].reshape(-1)]
    count = len(column)
    try:
        coords = [tuple(d.coords) + (d.core_on_chip,) for d in column]
    except AttributeError:
        return list(range(count))
    varying = [k for k in range(len(coords[0])) if len({c[k] for c in coords}) > 1]
    if len(varying) != 2:
        return list(range(count))
    sizes = [len({c[k] for c in coords}) for k in varying]
    if 2 not in sizes or sizes[0] * sizes[1] != count:
        return list(range(count))
    short, long = (varying[0], varying[1]) if sizes[0] == 2 else (varying[1], varying[0])
    low_short = min(c[short] for c in coords)
    lanes = [[], []]
    for index, c in enumerate(coords):
        lanes[0 if c[short] == low_short else 1].append((c[long], index))
    return [i for _, i in sorted(lanes[0])] + [i for _, i in sorted(lanes[1], reverse=True)]


def solution(mesh):
    placed = (
        P("seq", "tp"),
        P("seq", "tp"),
        P("seq", "tp"),
        P(None, None, "tp"),
        P("tp", None),
        P("tp", None),
        P(("seq", "tp"), None),
    )
    ring = ring_order(mesh)
    return jax.shard_map(
        functools.partial(per_device, ring=ring),
        mesh=mesh,
        in_specs=placed,
        out_specs=(
            P(("seq", "tp"), None),
            P("seq", "tp"),
            P("seq", "tp"),
            P("seq", "tp"),
            P("tp", "seq"),
        ),
        check_vma=False,
    )
```

```python
import functools

import jax
import jax.numpy as jnp
from jax import lax
from jax.experimental import pallas as pl
from jax.sharding import PartitionSpec as P


def passed_along(value, axis, steps):
    count = lax.axis_size(axis)
    leading, last = (max(0, -steps), min(count, count - steps))
    return lax.ppermute(value, axis, [(source, source + steps) for source in range(leading, last)])


def featurize(extended, feature_taps, out_rows):
    tap_span = feature_taps.shape[0]
    summed = jnp.zeros((out_rows,) + extended.shape[1:], jnp.float32)
    for offset in range(tap_span):
        first_row = tap_span - 1 - offset
        summed = summed + feature_taps[offset] * extended[first_row : first_row + out_rows].astype(
            jnp.float32
        )
    return summed


def spread_back(extended, feature_taps, out_rows):
    tap_span = feature_taps.shape[0]
    summed = jnp.zeros((out_rows,) + extended.shape[1:], jnp.float32)
    for offset in range(tap_span):
        summed = summed + feature_taps[offset] * extended[offset : offset + out_rows]
    return summed


def band_table(filter_taps, reverse=False):
    tap_count = filter_taps.shape[1]
    window_rows = 2 * tap_count
    lag_index = jnp.arange(tap_count)[:, None, None]
    out_index = jnp.arange(tap_count)[None, :, None]
    row_index = jnp.arange(window_rows)[None, None, :]
    if reverse:
        select = (row_index - out_index == lag_index).astype(jnp.bfloat16)
    else:
        select = (out_index + tap_count - row_index == lag_index).astype(jnp.bfloat16)
    select = select.reshape(tap_count, tap_count * window_rows)
    table = jnp.dot(filter_taps, select, preferred_element_type=jnp.float32)
    return table.astype(jnp.bfloat16).reshape(filter_taps.shape[0], tap_count, window_rows)


def band_mix(padded_rows, table, lane_tile=128):
    group_count, tap_count, window_rows = table.shape
    row_count = padded_rows.shape[0] - tap_count
    block_count = row_count // tap_count
    channels = padded_rows.shape[1]
    members = channels // group_count
    per_tile = lane_tile // members

    def body(table_ref, rows_ref, out_ref):
        lane_group = lax.broadcasted_iota(jnp.int32, (1, lane_tile), 1) // members
        rows = rows_ref[...]
        window = jnp.concatenate(
            [rows[n * tap_count : n * tap_count + window_rows] for n in range(block_count)], axis=1
        )
        mixed = [jnp.zeros((tap_count, lane_tile), jnp.float32) for _ in range(block_count)]
        for member in range(per_tile):
            part = jnp.dot(table_ref[member], window, preferred_element_type=jnp.float32)
            for n in range(block_count):
                mixed[n] = jnp.where(
                    lane_group == member, part[:, n * lane_tile : (n + 1) * lane_tile], mixed[n]
                )
        for n in range(block_count):
            out_ref[n * tap_count : (n + 1) * tap_count, :] = mixed[n]

    return pl.pallas_call(
        body,
        grid=(channels // lane_tile,),
        in_specs=[
            pl.BlockSpec((per_tile, tap_count, window_rows), lambda j: (j, 0, 0)),
            pl.BlockSpec((row_count + tap_count, lane_tile), lambda j: (0, j)),
        ],
        out_specs=pl.BlockSpec((row_count, lane_tile), lambda j: (0, j)),
        out_shape=jax.ShapeDtypeStruct((row_count, channels), jnp.float32),
    )(table, padded_rows)


def per_device(query_in, key_in, value_in, feature_taps, filter_taps, out_weight, cotangent, ring):
    row_count, channels = query_in.shape
    tap_count = filter_taps.shape[1]
    tap_span = feature_taps.shape[0]
    full_cotangent = lax.all_gather(cotangent, "tp", axis=0, tiled=True)
    inputs = (query_in, key_in, value_in)
    before = passed_along(
        jnp.stack([rows[row_count - tap_span + 1 :] for rows in inputs], axis=0), "seq", 1
    )
    query_feat, key_feat, value_feat = (
        featurize(jnp.concatenate([before[i], inputs[i]], axis=0), feature_taps[:, i], row_count)
        for i in range(3)
    )
    mix_rows = (key_feat * value_feat).astype(jnp.bfloat16)
    mix_before = passed_along(mix_rows[row_count - tap_count :], "seq", 1)
    padded_mix = jnp.concatenate([mix_before, mix_rows], axis=0)
    long_conv = band_mix(padded_mix, band_table(filter_taps))
    gated_rows = (query_feat * long_conv).astype(jnp.bfloat16)
    seq_count = lax.axis_size("seq")
    grad_scale = (row_count * seq_count) ** (-0.5)

    projected = []

    def project(state):
        gated_rows, out_weight = state
        projected.append(
            lax.psum_scatter(
                jnp.dot(gated_rows, out_weight, preferred_element_type=jnp.float32).astype(
                    jnp.bfloat16
                ),
                "tp",
                scatter_dimension=0,
                tiled=True,
            )
        )
        return out_weight

    def gate_back(out_weight):
        grad_gated = lax.dot_general(
            full_cotangent, out_weight, (((1,), (1,)), ((), ())), preferred_element_type=jnp.float32
        )
        grad_conv = (grad_gated * query_feat).astype(jnp.bfloat16)
        grad_query = grad_gated * long_conv
        conv_after = passed_along(grad_conv[:tap_count], "seq", -1)
        return (grad_conv, conv_after, grad_query, out_weight)

    def table_back(state):
        return state + (band_table(filter_taps, reverse=True),)

    def filter_back(state):
        grad_conv, conv_after, grad_query, out_weight, table = state
        grad_mix = band_mix(jnp.concatenate([grad_conv, conv_after], axis=0), table)
        grad_features = (grad_query, grad_mix * value_feat, grad_mix * key_feat)
        features_after = passed_along(
            jnp.stack([rows[: tap_span - 1] for rows in grad_features], axis=0).astype(jnp.bfloat16),
            "seq",
            -1,
        )
        return (grad_features, features_after, out_weight)

    def feature_back(first, last):
        def stage(state):
            grad_features, features_after, done = state
            grads = tuple(
                spread_back(
                    jnp.concatenate(
                        [grad_features[i], features_after[i].astype(jnp.float32)], axis=0
                    ),
                    feature_taps[:, i],
                    row_count,
                ).astype(jnp.bfloat16)
                for i in range(first, last)
            )
            return (grad_features, features_after, done + grads)

        return stage

    def finish(state):
        return state[2]

    def unpack(state):
        grad_features, features_after = state
        return (grad_features, features_after, ())

    def start_back(out_weight):
        return out_weight

    stages = [
        start_back,
        gate_back,
        table_back,
        filter_back,
        lambda state: (project((gated_rows, state[2])), state[:2])[1],
        lambda state: feature_back(0, 2)(unpack(state)),
        lambda state: finish(feature_back(2, 3)(state)),
    ]
    state, summed_grad = ring_reduce_scatter(
        gated_rows, full_cotangent, grad_scale, ring, stages, out_weight
    )
    return (projected[0],) + state + (summed_grad,)


def ring_reduce_scatter(gated_rows, full_cotangent, grad_scale, ring, stages, state):
    count = len(ring)
    width = full_cotangent.shape[1] // count
    half = width // 2
    place_of = [0] * count
    for place, member in enumerate(ring):
        place_of[member] = place
    seq_index = lax.axis_index("seq")
    place = sum(jnp.where(seq_index == member, place_of[member], 0) for member in range(count))
    forward = [(ring[i], ring[(i + 1) % count]) for i in range(count)]
    backward = [(ring[(i + 1) % count], ring[i]) for i in range(count)]
    def product(rows, columns):
        return (
            lax.dot_general(
                rows, columns, (((0,), (0,)), ((), ())), preferred_element_type=jnp.float32
            )
            * grad_scale
        ).astype(jnp.bfloat16)

    def column_of(step, direction):
        position = (place - direction * (1 + step)) % count
        owner = sum(jnp.where(position == i, ring[i], 0) for i in range(count))
        return owner * width + (0 if direction == 1 else half)

    def first_slice(direction):
        columns = lax.dynamic_slice_in_dim(full_cotangent, column_of(0, direction), half, 1)
        return product(gated_rows, columns).astype(jnp.float32)

    ahead = first_slice(1)
    behind = first_slice(-1)
    stages = list(stages)
    local_grad = None
    for step in range(1, count):
        sent_ahead = ahead.astype(jnp.bfloat16)
        sent_behind = behind.astype(jnp.bfloat16)
        sent_ahead, sent_behind, state, rows = lax.optimization_barrier(
            (sent_ahead, sent_behind, state, gated_rows)
        )
        ahead = lax.ppermute(sent_ahead, "seq", forward)
        behind = lax.ppermute(sent_behind, "seq", backward)
        if local_grad is None:
            local_grad = product(rows, full_cotangent)
        if stages:
            state = stages.pop(0)(state)
        ahead, behind, state, local_grad = lax.optimization_barrier(
            (ahead, behind, state, local_grad)
        )
        ahead = ahead.astype(jnp.float32) + lax.dynamic_slice_in_dim(
            local_grad, column_of(step, 1), half, 1
        ).astype(jnp.float32)
        behind = behind.astype(jnp.float32) + lax.dynamic_slice_in_dim(
            local_grad, column_of(step, -1), half, 1
        ).astype(jnp.float32)
    while stages:
        state = stages.pop(0)(state)
    return state, jnp.concatenate([ahead, behind], axis=1).astype(jnp.bfloat16)


def ring_order(mesh):
    axis = mesh.axis_names.index("seq")
    members = jnp.moveaxis(jnp.arange(mesh.devices.size).reshape(mesh.devices.shape), axis, 0)
    devices = mesh.devices.reshape(-1)
    column = [devices[int(i)] for i in members[:, 0].reshape(-1)]
    count = len(column)
    try:
        coords = [tuple(d.coords) + (d.core_on_chip,) for d in column]
    except AttributeError:
        return list(range(count))
    varying = [k for k in range(len(coords[0])) if len({c[k] for c in coords}) > 1]
    if len(varying) != 2:
        return list(range(count))
    sizes = [len({c[k] for c in coords}) for k in varying]
    if 2 not in sizes or sizes[0] * sizes[1] != count:
        return list(range(count))
    short, long = (varying[0], varying[1]) if sizes[0] == 2 else (varying[1], varying[0])
    low_short = min(c[short] for c in coords)
    lanes = [[], []]
    for index, c in enumerate(coords):
        lanes[0 if c[short] == low_short else 1].append((c[long], index))
    return [i for _, i in sorted(lanes[0])] + [i for _, i in sorted(lanes[1], reverse=True)]


def solution(mesh):
    placed = (
        P("seq", "tp"),
        P("seq", "tp"),
        P("seq", "tp"),
        P(None, None, "tp"),
        P("tp", None),
        P("tp", None),
        P(("seq", "tp"), None),
    )
    ring = ring_order(mesh)
    return jax.shard_map(
        functools.partial(per_device, ring=ring),
        mesh=mesh,
        in_specs=placed,
        out_specs=(
            P(("seq", "tp"), None),
            P("seq", "tp"),
            P("seq", "tp"),
            P("seq", "tp"),
            P("tp", "seq"),
        ),
        check_vma=False,
    )
```

```python
import functools

import jax
import jax.numpy as jnp
from jax import lax
from jax.experimental import pallas as pl
from jax.sharding import PartitionSpec as P


def passed_along(value, axis, steps):
    count = lax.axis_size(axis)
    leading, last = (max(0, -steps), min(count, count - steps))
    return lax.ppermute(value, axis, [(source, source + steps) for source in range(leading, last)])


def featurize(extended, feature_taps, out_rows):
    tap_span = feature_taps.shape[0]
    summed = jnp.zeros((out_rows,) + extended.shape[1:], jnp.float32)
    for offset in range(tap_span):
        first_row = tap_span - 1 - offset
        summed = summed + feature_taps[offset] * extended[first_row : first_row + out_rows].astype(
            jnp.float32
        )
    return summed


def spread_back(extended, feature_taps, out_rows):
    tap_span = feature_taps.shape[0]
    summed = jnp.zeros((out_rows,) + extended.shape[1:], jnp.float32)
    for offset in range(tap_span):
        summed = summed + feature_taps[offset] * extended[offset : offset + out_rows]
    return summed


def band_table(filter_taps, reverse=False):
    tap_count = filter_taps.shape[1]
    window_rows = 2 * tap_count
    lag_index = jnp.arange(tap_count)[:, None, None]
    out_index = jnp.arange(tap_count)[None, :, None]
    row_index = jnp.arange(window_rows)[None, None, :]
    if reverse:
        select = (row_index - out_index == lag_index).astype(jnp.bfloat16)
    else:
        select = (out_index + tap_count - row_index == lag_index).astype(jnp.bfloat16)
    select = select.reshape(tap_count, tap_count * window_rows)
    table = jnp.dot(filter_taps, select, preferred_element_type=jnp.float32)
    return table.astype(jnp.bfloat16).reshape(filter_taps.shape[0], tap_count, window_rows)


def band_mix(padded_rows, table, lane_tile=128):
    group_count, tap_count, window_rows = table.shape
    row_count = padded_rows.shape[0] - tap_count
    block_count = row_count // tap_count
    channels = padded_rows.shape[1]
    members = channels // group_count
    per_tile = lane_tile // members

    def body(table_ref, rows_ref, out_ref):
        lane_group = lax.broadcasted_iota(jnp.int32, (1, lane_tile), 1) // members
        rows = rows_ref[...]
        window = jnp.concatenate(
            [rows[n * tap_count : n * tap_count + window_rows] for n in range(block_count)], axis=1
        )
        stacked = table_ref[...].reshape(per_tile * tap_count, window_rows)
        part = jnp.dot(stacked, window, preferred_element_type=jnp.float32)
        mixed = [jnp.zeros((tap_count, lane_tile), jnp.float32) for _ in range(block_count)]
        for member in range(per_tile):
            rows_of = slice(member * tap_count, (member + 1) * tap_count)
            for n in range(block_count):
                mixed[n] = jnp.where(
                    lane_group == member,
                    part[rows_of, n * lane_tile : (n + 1) * lane_tile],
                    mixed[n],
                )
        for n in range(block_count):
            out_ref[n * tap_count : (n + 1) * tap_count, :] = mixed[n]

    return pl.pallas_call(
        body,
        grid=(channels // lane_tile,),
        in_specs=[
            pl.BlockSpec((per_tile, tap_count, window_rows), lambda j: (j, 0, 0)),
            pl.BlockSpec((row_count + tap_count, lane_tile), lambda j: (0, j)),
        ],
        out_specs=pl.BlockSpec((row_count, lane_tile), lambda j: (0, j)),
        out_shape=jax.ShapeDtypeStruct((row_count, channels), jnp.float32),
    )(table, padded_rows)


def per_device(query_in, key_in, value_in, feature_taps, filter_taps, out_weight, cotangent, ring):
    row_count, channels = query_in.shape
    tap_count = filter_taps.shape[1]
    tap_span = feature_taps.shape[0]
    full_cotangent = lax.all_gather(cotangent, "tp", axis=0, tiled=True)
    inputs = (query_in, key_in, value_in)
    before = passed_along(
        jnp.stack([rows[row_count - tap_span + 1 :] for rows in inputs], axis=0), "seq", 1
    )
    query_feat, key_feat, value_feat = (
        featurize(jnp.concatenate([before[i], inputs[i]], axis=0), feature_taps[:, i], row_count)
        for i in range(3)
    )
    mix_rows = (key_feat * value_feat).astype(jnp.bfloat16)
    mix_before = passed_along(mix_rows[row_count - tap_count :], "seq", 1)
    padded_mix = jnp.concatenate([mix_before, mix_rows], axis=0)
    long_conv = band_mix(padded_mix, band_table(filter_taps))
    gated_rows = (query_feat * long_conv).astype(jnp.bfloat16)
    seq_count = lax.axis_size("seq")
    grad_scale = (row_count * seq_count) ** (-0.5)

    projected = []

    def project(state):
        gated_rows, out_weight = state
        projected.append(
            lax.psum_scatter(
                jnp.dot(gated_rows, out_weight, preferred_element_type=jnp.float32).astype(
                    jnp.bfloat16
                ),
                "tp",
                scatter_dimension=0,
                tiled=True,
            )
        )
        return out_weight

    def gate_back(out_weight):
        grad_gated = lax.dot_general(
            full_cotangent, out_weight, (((1,), (1,)), ((), ())), preferred_element_type=jnp.float32
        )
        grad_conv = (grad_gated * query_feat).astype(jnp.bfloat16)
        grad_query = grad_gated * long_conv
        conv_after = passed_along(grad_conv[:tap_count], "seq", -1)
        return (grad_conv, conv_after, grad_query)

    def table_back(state):
        return state + (band_table(filter_taps, reverse=True),)

    def filter_back(state):
        grad_conv, conv_after, grad_query, table = state
        grad_mix = band_mix(jnp.concatenate([grad_conv, conv_after], axis=0), table)
        grad_features = (grad_query, grad_mix * value_feat, grad_mix * key_feat)
        features_after = passed_along(
            jnp.stack([rows[: tap_span - 1] for rows in grad_features], axis=0).astype(jnp.bfloat16),
            "seq",
            -1,
        )
        return (grad_features, features_after)

    def feature_back(first, last):
        def stage(state):
            grad_features, features_after, done = state
            grads = tuple(
                spread_back(
                    jnp.concatenate(
                        [grad_features[i], features_after[i].astype(jnp.float32)], axis=0
                    ),
                    feature_taps[:, i],
                    row_count,
                ).astype(jnp.bfloat16)
                for i in range(first, last)
            )
            return (grad_features, features_after, done + grads)

        return stage

    def finish(state):
        return state[2]

    def unpack(state):
        grad_features, features_after = state
        return (grad_features, features_after, ())

    stages = [
        project,
        gate_back,
        table_back,
        filter_back,
        lambda state: feature_back(0, 1)(unpack(state)),
        feature_back(1, 3),
        finish,
    ]
    state, summed_grad = ring_reduce_scatter(
        gated_rows, full_cotangent, grad_scale, ring, stages, (gated_rows, out_weight)
    )
    return (projected[0],) + state + (summed_grad,)


def ring_reduce_scatter(gated_rows, full_cotangent, grad_scale, ring, stages, state):
    count = len(ring)
    width = full_cotangent.shape[1] // count
    half = width // 2
    place_of = [0] * count
    for place, member in enumerate(ring):
        place_of[member] = place
    seq_index = lax.axis_index("seq")
    place = sum(jnp.where(seq_index == member, place_of[member], 0) for member in range(count))
    forward = [(ring[i], ring[(i + 1) % count]) for i in range(count)]
    backward = [(ring[(i + 1) % count], ring[i]) for i in range(count)]
    local_grad = (
        lax.dot_general(
            gated_rows, full_cotangent, (((0,), (0,)), ((), ())), preferred_element_type=jnp.float32
        )
        * grad_scale
    ).astype(jnp.bfloat16)

    def contribution(step, direction):
        position = (place - direction * (1 + step)) % count
        owner = sum(jnp.where(position == i, ring[i], 0) for i in range(count))
        first = owner * width + (0 if direction == 1 else half)
        return lax.dynamic_slice_in_dim(local_grad, first, half, 1)

    ahead = contribution(0, 1)
    behind = contribution(0, -1)
    stages = list(stages)
    for step in range(1, count):
        sent_ahead = ahead.astype(jnp.bfloat16)
        sent_behind = behind.astype(jnp.bfloat16)
        if stages:
            sent_ahead, sent_behind, state = lax.optimization_barrier(
                (sent_ahead, sent_behind, state)
            )
        ahead = lax.ppermute(sent_ahead, "seq", forward)
        behind = lax.ppermute(sent_behind, "seq", backward)
        if stages:
            state = stages.pop(0)(state)
            ahead, behind, state = lax.optimization_barrier((ahead, behind, state))
        ahead = ahead.astype(jnp.float32) + contribution(step, 1).astype(jnp.float32)
        behind = behind.astype(jnp.float32) + contribution(step, -1).astype(jnp.float32)
    while stages:
        state = stages.pop(0)(state)
    return state, jnp.concatenate([ahead, behind], axis=1).astype(jnp.bfloat16)


def ring_order(mesh):
    axis = mesh.axis_names.index("seq")
    members = jnp.moveaxis(jnp.arange(mesh.devices.size).reshape(mesh.devices.shape), axis, 0)
    devices = mesh.devices.reshape(-1)
    column = [devices[int(i)] for i in members[:, 0].reshape(-1)]
    count = len(column)
    try:
        coords = [tuple(d.coords) + (d.core_on_chip,) for d in column]
    except AttributeError:
        return list(range(count))
    varying = [k for k in range(len(coords[0])) if len({c[k] for c in coords}) > 1]
    if len(varying) != 2:
        return list(range(count))
    sizes = [len({c[k] for c in coords}) for k in varying]
    if 2 not in sizes or sizes[0] * sizes[1] != count:
        return list(range(count))
    short, long = (varying[0], varying[1]) if sizes[0] == 2 else (varying[1], varying[0])
    low_short = min(c[short] for c in coords)
    lanes = [[], []]
    for index, c in enumerate(coords):
        lanes[0 if c[short] == low_short else 1].append((c[long], index))
    return [i for _, i in sorted(lanes[0])] + [i for _, i in sorted(lanes[1], reverse=True)]


def solution(mesh):
    placed = (
        P("seq", "tp"),
        P("seq", "tp"),
        P("seq", "tp"),
        P(None, None, "tp"),
        P("tp", None),
        P("tp", None),
        P(("seq", "tp"), None),
    )
    ring = ring_order(mesh)
    return jax.shard_map(
        functools.partial(per_device, ring=ring),
        mesh=mesh,
        in_specs=placed,
        out_specs=(
            P(("seq", "tp"), None),
            P("seq", "tp"),
            P("seq", "tp"),
            P("seq", "tp"),
            P("tp", "seq"),
        ),
        check_vma=False,
    )
```

```python
import functools

import jax
import jax.numpy as jnp
from jax import lax
from jax.experimental import pallas as pl
from jax.sharding import PartitionSpec as P


def passed_along(value, axis, steps):
    count = lax.axis_size(axis)
    leading, last = (max(0, -steps), min(count, count - steps))
    return lax.ppermute(value, axis, [(source, source + steps) for source in range(leading, last)])


def featurize(extended, feature_taps, out_rows):
    tap_span = feature_taps.shape[0]
    summed = jnp.zeros((out_rows,) + extended.shape[1:], jnp.float32)
    for offset in range(tap_span):
        first_row = tap_span - 1 - offset
        summed = summed + feature_taps[offset] * extended[first_row : first_row + out_rows].astype(
            jnp.float32
        )
    return summed


def spread_back(extended, feature_taps, out_rows):
    tap_span = feature_taps.shape[0]
    summed = jnp.zeros((out_rows,) + extended.shape[1:], jnp.float32)
    for offset in range(tap_span):
        summed = summed + feature_taps[offset] * extended[offset : offset + out_rows]
    return summed


def band_table(filter_taps, reverse=False):
    tap_count = filter_taps.shape[1]
    window_rows = 2 * tap_count
    lag_index = jnp.arange(tap_count)[:, None, None]
    out_index = jnp.arange(tap_count)[None, :, None]
    row_index = jnp.arange(window_rows)[None, None, :]
    if reverse:
        select = (row_index - out_index == lag_index).astype(jnp.bfloat16)
    else:
        select = (out_index + tap_count - row_index == lag_index).astype(jnp.bfloat16)
    select = select.reshape(tap_count, tap_count * window_rows)
    table = jnp.dot(filter_taps, select, preferred_element_type=jnp.float32)
    return table.astype(jnp.bfloat16).reshape(filter_taps.shape[0], tap_count, window_rows)


def band_mix(padded_rows, table, lane_tile=256):
    group_count, tap_count, window_rows = table.shape
    row_count = padded_rows.shape[0] - tap_count
    block_count = row_count // tap_count
    channels = padded_rows.shape[1]
    members = channels // group_count
    per_tile = lane_tile // members

    def body(table_ref, rows_ref, out_ref):
        lane_group = lax.broadcasted_iota(jnp.int32, (1, lane_tile), 1) // members
        rows = rows_ref[...]
        window = jnp.concatenate(
            [rows[n * tap_count : n * tap_count + window_rows] for n in range(block_count)], axis=1
        )
        stacked = table_ref[...].reshape(per_tile * tap_count, window_rows)
        part = jnp.dot(stacked, window, preferred_element_type=jnp.float32)
        mixed = [jnp.zeros((tap_count, lane_tile), jnp.float32) for _ in range(block_count)]
        for member in range(per_tile):
            rows_of = slice(member * tap_count, (member + 1) * tap_count)
            for n in range(block_count):
                mixed[n] = jnp.where(
                    lane_group == member,
                    part[rows_of, n * lane_tile : (n + 1) * lane_tile],
                    mixed[n],
                )
        for n in range(block_count):
            out_ref[n * tap_count : (n + 1) * tap_count, :] = mixed[n]

    return pl.pallas_call(
        body,
        grid=(channels // lane_tile,),
        in_specs=[
            pl.BlockSpec((per_tile, tap_count, window_rows), lambda j: (j, 0, 0)),
            pl.BlockSpec((row_count + tap_count, lane_tile), lambda j: (0, j)),
        ],
        out_specs=pl.BlockSpec((row_count, lane_tile), lambda j: (0, j)),
        out_shape=jax.ShapeDtypeStruct((row_count, channels), jnp.float32),
    )(table, padded_rows)


def per_device(query_in, key_in, value_in, feature_taps, filter_taps, out_weight, cotangent, ring):
    row_count, channels = query_in.shape
    tap_count = filter_taps.shape[1]
    tap_span = feature_taps.shape[0]
    full_cotangent = lax.all_gather(cotangent, "tp", axis=0, tiled=True)
    inputs = (query_in, key_in, value_in)
    before = passed_along(
        jnp.stack([rows[row_count - tap_span + 1 :] for rows in inputs], axis=0), "seq", 1
    )
    query_feat, key_feat, value_feat = (
        featurize(jnp.concatenate([before[i], inputs[i]], axis=0), feature_taps[:, i], row_count)
        for i in range(3)
    )
    mix_rows = (key_feat * value_feat).astype(jnp.bfloat16)
    mix_before = passed_along(mix_rows[row_count - tap_count :], "seq", 1)
    padded_mix = jnp.concatenate([mix_before, mix_rows], axis=0)
    long_conv = band_mix(padded_mix, band_table(filter_taps))
    gated_rows = (query_feat * long_conv).astype(jnp.bfloat16)
    seq_count = lax.axis_size("seq")
    grad_scale = (row_count * seq_count) ** (-0.5)

    projected = []

    def project(state):
        gated_rows, out_weight = state
        projected.append(
            lax.psum_scatter(
                jnp.dot(gated_rows, out_weight, preferred_element_type=jnp.float32).astype(
                    jnp.bfloat16
                ),
                "tp",
                scatter_dimension=0,
                tiled=True,
            )
        )
        return out_weight

    def gate_back(out_weight):
        grad_gated = lax.dot_general(
            full_cotangent, out_weight, (((1,), (1,)), ((), ())), preferred_element_type=jnp.float32
        )
        grad_conv = (grad_gated * query_feat).astype(jnp.bfloat16)
        grad_query = grad_gated * long_conv
        conv_after = passed_along(grad_conv[:tap_count], "seq", -1)
        return (grad_conv, conv_after, grad_query)

    def table_back(state):
        return state + (band_table(filter_taps, reverse=True),)

    def filter_back(state):
        grad_conv, conv_after, grad_query, table = state
        grad_mix = band_mix(jnp.concatenate([grad_conv, conv_after], axis=0), table)
        grad_features = (grad_query, grad_mix * value_feat, grad_mix * key_feat)
        features_after = passed_along(
            jnp.stack([rows[: tap_span - 1] for rows in grad_features], axis=0).astype(jnp.bfloat16),
            "seq",
            -1,
        )
        return (grad_features, features_after)

    def feature_back(first, last):
        def stage(state):
            grad_features, features_after, done = state
            grads = tuple(
                spread_back(
                    jnp.concatenate(
                        [grad_features[i], features_after[i].astype(jnp.float32)], axis=0
                    ),
                    feature_taps[:, i],
                    row_count,
                ).astype(jnp.bfloat16)
                for i in range(first, last)
            )
            return (grad_features, features_after, done + grads)

        return stage

    def finish(state):
        return state[2]

    def unpack(state):
        grad_features, features_after = state
        return (grad_features, features_after, ())

    stages = [
        project,
        gate_back,
        table_back,
        filter_back,
        lambda state: feature_back(0, 1)(unpack(state)),
        feature_back(1, 3),
        finish,
    ]
    state, summed_grad = ring_reduce_scatter(
        gated_rows, full_cotangent, grad_scale, ring, stages, (gated_rows, out_weight)
    )
    return (projected[0],) + state + (summed_grad,)


def ring_reduce_scatter(gated_rows, full_cotangent, grad_scale, ring, stages, state):
    count = len(ring)
    width = full_cotangent.shape[1] // count
    half = width // 2
    place_of = [0] * count
    for place, member in enumerate(ring):
        place_of[member] = place
    seq_index = lax.axis_index("seq")
    place = sum(jnp.where(seq_index == member, place_of[member], 0) for member in range(count))
    forward = [(ring[i], ring[(i + 1) % count]) for i in range(count)]
    backward = [(ring[(i + 1) % count], ring[i]) for i in range(count)]
    local_grad = (
        lax.dot_general(
            gated_rows, full_cotangent, (((0,), (0,)), ((), ())), preferred_element_type=jnp.float32
        )
        * grad_scale
    ).astype(jnp.bfloat16)

    def contribution(step, direction):
        position = (place - direction * (1 + step)) % count
        owner = sum(jnp.where(position == i, ring[i], 0) for i in range(count))
        first = owner * width + (0 if direction == 1 else half)
        return lax.dynamic_slice_in_dim(local_grad, first, half, 1)

    ahead = contribution(0, 1)
    behind = contribution(0, -1)
    stages = list(stages)
    for step in range(1, count):
        sent_ahead = ahead.astype(jnp.bfloat16)
        sent_behind = behind.astype(jnp.bfloat16)
        if stages:
            sent_ahead, sent_behind, state = lax.optimization_barrier(
                (sent_ahead, sent_behind, state)
            )
        ahead = lax.ppermute(sent_ahead, "seq", forward)
        behind = lax.ppermute(sent_behind, "seq", backward)
        if stages:
            state = stages.pop(0)(state)
            ahead, behind, state = lax.optimization_barrier((ahead, behind, state))
        ahead = ahead.astype(jnp.float32) + contribution(step, 1).astype(jnp.float32)
        behind = behind.astype(jnp.float32) + contribution(step, -1).astype(jnp.float32)
    while stages:
        state = stages.pop(0)(state)
    return state, jnp.concatenate([ahead, behind], axis=1).astype(jnp.bfloat16)


def ring_order(mesh):
    axis = mesh.axis_names.index("seq")
    members = jnp.moveaxis(jnp.arange(mesh.devices.size).reshape(mesh.devices.shape), axis, 0)
    devices = mesh.devices.reshape(-1)
    column = [devices[int(i)] for i in members[:, 0].reshape(-1)]
    count = len(column)
    try:
        coords = [tuple(d.coords) + (d.core_on_chip,) for d in column]
    except AttributeError:
        return list(range(count))
    varying = [k for k in range(len(coords[0])) if len({c[k] for c in coords}) > 1]
    if len(varying) != 2:
        return list(range(count))
    sizes = [len({c[k] for c in coords}) for k in varying]
    if 2 not in sizes or sizes[0] * sizes[1] != count:
        return list(range(count))
    short, long = (varying[0], varying[1]) if sizes[0] == 2 else (varying[1], varying[0])
    low_short = min(c[short] for c in coords)
    lanes = [[], []]
    for index, c in enumerate(coords):
        lanes[0 if c[short] == low_short else 1].append((c[long], index))
    return [i for _, i in sorted(lanes[0])] + [i for _, i in sorted(lanes[1], reverse=True)]


def solution(mesh):
    placed = (
        P("seq", "tp"),
        P("seq", "tp"),
        P("seq", "tp"),
        P(None, None, "tp"),
        P("tp", None),
        P("tp", None),
        P(("seq", "tp"), None),
    )
    ring = ring_order(mesh)
    return jax.shard_map(
        functools.partial(per_device, ring=ring),
        mesh=mesh,
        in_specs=placed,
        out_specs=(
            P(("seq", "tp"), None),
            P("seq", "tp"),
            P("seq", "tp"),
            P("seq", "tp"),
            P("tp", "seq"),
        ),
        check_vma=False,
    )
```
